32 devices in a mesh: dp: 2 (over x), seq: 16 (over z, y, core).
Axes of the slice: x: 2, y: 2, z: 4, core: 2. Of those that a mesh axis runs over, the one named last changes fastest.
Arguments:
- frames: bfloat16 [2, 16, 64, 48, 128], P('dp', None, 'seq'), may hold values from -6 to 6
- frame_counts: int32 [2, 4], P('dp'), may hold values from 1 to 12, 16 in all within a row
- clip_group: int32 [2, 4], P('dp'), may hold values 0 or 1
- timesteps: int32 [2, 4], P('dp'), may hold values from 0 to 999
- owner_map: int32 [2, 16, 192, 1], P('dp', 'seq'), may hold values from 0 to 15; in each aligned block of 192 rows (0 to 191, 192 to 383, ..., all dimensions but the last counted through in order) at most 18 rows name the same one
- conv_weight: bfloat16 [3, 3, 3, 128, 128], replicated, may hold values from -0.109375 to 0.109375
- w_latent: bfloat16 [2048, 64], replicated, may hold values from -0.125 to 0.125
- hidden: bfloat16 [2, 4608, 3072], P('dp', 'seq'), may hold values from -6 to 6
- noise: float32 [2, 4608, 64], P('dp', 'seq'), may hold values from -6 to 6
- teacher: float32 [2, 4608, 64], P('dp', 'seq'), may hold values from -6 to 6
- w_out: bfloat16 [3072, 64], replicated, may hold values from -0.109375 to 0.109375
Outputs:
- latent: bfloat16 [2, 16, 16, 768], P('dp', None, 'seq')
- clip_loss: float32 [2, 4], P('dp')
- grad_out: float32 [3072, 64], P('seq')
The draws below stay inside these ranges and needn't reach their ends.
Inputs may be any that keep to these rules, and one draw needn't show every extreme that they name: `owner_map`: among the tokens of one device no owner is named more than 18 times, a bound that some block reaches. `frame_counts`: the counts of a group sum to 16; the largest is exactly 12.
All inputs are finite; a program needn't handle non-finite values. No bound on the sum of `clip_group` on one device may be relied on, other than what follows from the above.
Results may differ from the reference program's by a relative error of at most 0.0055.
Values may be sent and summed in bfloat16 or wider, within the bound.
No kernel may reach another device: no remote copies, remote signals or barrier semaphores. Data moves between devices by JAX's collectives and lax.ppermute only.
A program may use at most 64 MiB of HBM per device.

```python
import math
import jax
import jax.numpy as jnp
import numpy as np
from jax import lax

D = 3072
C = 128
LAT = 64
FRAMES = 16
CLIPS = 4
W = 48
MOST_FR = 12
H = 64
RT = 1
WT = 12
TOK_SRC = 192
TPF = 192
CAP = 18
SLOTS = 288
N_DP = 2
N_SEQ = 16


def touch_ends(entries, own_key, low, top_value):
    extent = entries.shape
    place = [jax.random.randint(jax.random.fold_in(own_key, axis), (), 0, extent[axis]) for axis in range(len(extent))]
    entries = entries.at[tuple(place)].set(low)
    longest = extent.index(max(extent))
    place[longest] = (place[longest] + 1) % extent[longest]
    return entries.at[tuple(place)].set(top_value)


def block_scale(stream_key, dims, shards, low, largest):
    gain = 1.0
    for dim, parts in shards:
        steps = jax.random.uniform(jax.random.fold_in(jax.random.fold_in(stream_key, 6), dim), (parts,), jnp.float32, low / len(shards), largest / len(shards))
        gain = gain * jnp.repeat(jnp.exp(steps), dims[dim] // parts).reshape((-1,) + (1,) * (len(dims) - 1 - dim))
    return gain


def split_up(count, total, most, slope):
    portions = [(1 << 20) // math.isqrt(rank ** slope) + 1 for rank in range(2, count + 1)]
    surplus, holding = total - most - (count - 1), [1] * (count - 1)
    while surplus > 0:
        candidates = [i for i in range(count - 1) if holding[i] < most]
        mass, remaining = sum([portions[i] for i in candidates]), surplus
        for i in candidates:
            more = min(most - holding[i], max(1, remaining * portions[i] // mass), surplus)
            holding[i] = holding[i] + more
            surplus = surplus - more
    return np.array([most] + holding)


def uneven_parts(key, amount, total, most, skew):
    if amount == 2:
        one = jax.random.randint(key, (), max(1, total - most), min(most, total - 1) + 1)
        return jnp.stack([one, total - one])
    sizes = jnp.asarray(split_up(amount, total, most, skew), jnp.int32)
    pairs = (amount - 1) // 2
    source_of, taker = sizes[1:1 + 2 * pairs:2], sizes[2:2 + 2 * pairs:2]
    room = jnp.minimum(source_of - 1, most - taker)
    moved = jax.random.randint(jax.random.fold_in(key, 1), (pairs,), 0, 1 << 20) % (room + 1)
    sizes = sizes.at[1:1 + 2 * pairs:2].set(source_of - moved).at[2:2 + 2 * pairs:2].set(taker + moved)
    return sizes[jax.random.permutation(jax.random.fold_in(key, 2), amount)]


def assign_block(own_key, own, number, rows, count, top, limit, skew):
    ranking = jax.random.permutation(own_key, count)
    crowded, ordinary = load_shares(count, rows * top, limit, skew, True), load_shares(count, rows * top, limit, skew, False)
    places = jnp.arange(count)

    def named(tallies, rotation):
        used = int((tallies > 0).sum())
        fixed = max(1, used // 4)
        moved = fixed + (places - fixed + rotation * (used - fixed)) % max(1, count - fixed)
        return jnp.zeros((count,), jnp.int32).at[ranking[jnp.where(places < fixed, places, moved)]].set(jnp.asarray(tallies, jnp.int32))

    tallies = jnp.where(number % 4 == 0, named(crowded, number // 4), named(ordinary, number - number // 4 - 1))
    mixed = jax.random.permutation(jax.random.fold_in(own, 3), count)
    source_of, taker = mixed[0:count // 2 * 2:2], mixed[1:count // 2 * 2:2]
    margin = jnp.minimum(tallies[source_of] - 1, limit - tallies[taker]) // 2
    margin = jnp.where((source_of == ranking[0]) | (taker == ranking[0]) | (tallies[taker] == 0), 0, jnp.maximum(margin, 0))
    moved = jax.random.randint(jax.random.fold_in(own, 4), (count // 2,), 0, 1 << 20) % (margin + 1)
    tallies = tallies.at[source_of].add(-moved).at[taker].add(moved)
    items = jnp.searchsorted(jnp.cumsum(tallies), jnp.arange(rows * top), side="right").astype(jnp.int32)
    table = items.reshape(top, rows).T
    table = table[jax.random.permutation(jax.random.fold_in(own, 1), rows)]
    rotation = jax.random.randint(jax.random.fold_in(own, 2), (rows, 1), 0, top)
    return jnp.take_along_axis(table, (jnp.arange(top)[None, :] + rotation) % top, axis=1)


def load_shares(number_of, total, limit, skew, full):
    portions = [(1 << 20) // math.isqrt(standing ** skew) + 1 for standing in range(1, number_of + 1)]
    largest = limit if full else min(limit, max(-(-total // number_of), total * portions[0] // sum(portions)))
    least = 1 if total - largest >= number_of - 1 else 0
    given, rest = [largest] + [least] * (number_of - 1), total - largest - least * (number_of - 1)
    while rest > 0:
        candidates = [i for i in range(1, number_of) if given[i] < largest] or [i for i in range(1, number_of) if given[i] < limit]
        whole, left = sum([portions[i] for i in candidates]), rest
        for i in candidates:
            extra = min(limit - given[i], max(1, left * portions[i] // whole), rest)
            given[i] = given[i] + extra
            rest = rest - extra
    return np.array(given)


def gaussian(rng, shape, scale, limit, pieces=(), kind=jnp.bfloat16):
    entries = scale * jax.random.normal(rng, shape, jnp.float32)
    if pieces:
        entries = entries * block_scale(rng, shape, pieces, -0.22, 0.18)
    return jnp.clip(entries, -limit, limit).astype(kind)


def setup_inputs(seed: int = 0) -> dict:
    arg_keys = jax.random.split(jax.random.key(seed), 12)
    frames = gaussian(arg_keys[0], (N_DP, FRAMES, H, W, C), 1.0, 6.0, ((0, 2), (2, 16)))
    frame_counts = jax.vmap(lambda own: uneven_parts(own, CLIPS, FRAMES, MOST_FR, 2))(jax.random.split(arg_keys[1], N_DP)).reshape((N_DP, CLIPS)).astype(jnp.int32)
    clip_group = touch_ends((jax.random.randint(arg_keys[2], (N_DP, CLIPS), 0, 2) < 1).astype(jnp.int32), jax.random.fold_in(arg_keys[2], 1), 0, 1)
    timesteps = touch_ends(jax.random.randint(arg_keys[3], (N_DP, CLIPS), 0, 1000), jax.random.fold_in(arg_keys[3], 1), 0, 999).astype(jnp.int32)
    owner_map_keys = jax.random.split(jax.random.fold_in(arg_keys[4], 1), N_DP * N_SEQ * TOK_SRC // TOK_SRC)
    owner_map_turns = jax.random.permutation(jax.random.fold_in(arg_keys[4], 3), N_DP * N_SEQ * TOK_SRC // TOK_SRC)
    owner_map = jax.vmap(lambda own, number: assign_block(jax.random.fold_in(arg_keys[4], 2), own, number, TOK_SRC, N_SEQ, 1, CAP, 2))(owner_map_keys, owner_map_turns).reshape((N_DP, N_SEQ, TOK_SRC, 1))
    conv_weight = gaussian(arg_keys[5], (3, 3, 3, C, C), (27 * C) ** -0.5, 0.109375)
    w_latent = gaussian(arg_keys[6], (16 * C, LAT), (16 * C) ** -0.5, 0.125)
    hidden = gaussian(arg_keys[7], (N_DP, N_SEQ * SLOTS, D), 1.0, 6.0, ((0, 2), (1, 16)))
    noise = gaussian(arg_keys[8], (N_DP, N_SEQ * SLOTS, LAT), 1.0, 6.0, ((0, 2), (1, 16)), jnp.float32)
    teacher = gaussian(arg_keys[9], (N_DP, N_SEQ * SLOTS, LAT), 1.0, 6.0, ((0, 2), (1, 16)), jnp.float32)
    w_out = gaussian(arg_keys[10], (D, LAT), D ** -0.5, 0.109375)
    return dict(frames=frames, frame_counts=frame_counts, clip_group=clip_group, timesteps=timesteps, owner_map=owner_map, conv_weight=conv_weight, w_latent=w_latent, hidden=hidden, noise=noise, teacher=teacher, w_out=w_out)


def clip_starts(frame_counts):
    ends = jnp.cumsum(frame_counts).astype(jnp.int32)
    index = jnp.arange(FRAMES).astype(jnp.int32)
    clip_of = lax.optimization_barrier(jnp.sum((index[:, None] >= ends[None, :]).astype(jnp.int32), axis=1)).astype(jnp.int32)
    hot = (clip_of[:, None] == jnp.arange(CLIPS).astype(jnp.int32)[None, :]).astype(jnp.int32)
    starts = lax.optimization_barrier(jnp.sum(hot * (ends - frame_counts)[None, :], axis=1)).astype(jnp.int32)
    return (clip_of, starts, index)

def encode_group(frames, conv_weight, w_latent, frame_counts):
    clip_of, starts, index = clip_starts(frame_counts)
    padded = jnp.pad(frames, ((2, 0), (1, 1), (1, 1), (0, 0)))
    total = jnp.zeros((FRAMES, H * W, C), jnp.float32)
    for lag in range(3):
        part = jnp.zeros((FRAMES * H * W, C), jnp.float32)
        for i in range(3):
            for j in range(3):
                piece = padded[2 - lag:2 - lag + FRAMES, i:i + H, j:j + W, :].reshape(-1, C)
                part = part + jnp.dot(piece, conv_weight[lag, i, j], preferred_element_type=jnp.float32)
        keep = (index - lag >= starts).astype(jnp.float32)
        total = total + part.reshape(FRAMES, H * W, C) * keep[:, None, None]
    conv = total.reshape(FRAMES, H, W, C)
    cells = (frames.astype(jnp.float32) + jax.nn.silu(conv)).astype(jnp.bfloat16)
    patches = cells.reshape(FRAMES, H // 4, 4, W // 4, 4, C).transpose(0, 1, 3, 2, 4, 5).reshape(-1, 16 * C)
    tokens = jnp.dot(patches, w_latent, preferred_element_type=jnp.float32).astype(jnp.bfloat16)
    return (tokens.reshape(FRAMES, H // 4, W // 4, LAT), clip_of)

def reference(frames, frame_counts, clip_group, timesteps, owner_map, conv_weight, w_latent, hidden, noise, teacher, w_out):
    latents = []
    losses = []
    grad_out = jnp.zeros((D, LAT), jnp.float32)
    for group in range(N_DP):
        counts = frame_counts[group]
        lat, clip_of = encode_group(frames[group], conv_weight, w_latent, counts)
        latents.append(lat.reshape(FRAMES, H // 4, WT * LAT))
        source = lat.reshape(FRAMES, N_SEQ, RT, WT, LAT).transpose(1, 0, 2, 3, 4).reshape(N_SEQ, TOK_SRC, LAT)
        tok_clip = jnp.repeat(clip_of, RT * WT).astype(jnp.int32)
        owners = owner_map[group, :, :, 0].astype(jnp.int32)
        hot = (owners[:, :, None] == jnp.arange(N_SEQ).astype(jnp.int32)[None, None, :]).astype(jnp.int32)
        rank = (lax.optimization_barrier(jnp.sum(jnp.cumsum(hot, axis=1) * hot, axis=2)) - 1).astype(jnp.int32)
        dest = owners * SLOTS + jnp.arange(N_SEQ).astype(jnp.int32)[:, None] * CAP + rank
        dest = dest.reshape(-1).astype(jnp.int32)
        x0 = jnp.zeros((N_SEQ * SLOTS, LAT), jnp.float32).at[dest].set(source.reshape(-1, LAT).astype(jnp.float32))
        tag = jnp.full((N_SEQ * SLOTS,), -1, jnp.int32).at[dest].set(jnp.tile(tok_clip, N_SEQ))
        kind = clip_group[group].astype(jnp.float32)
        coef = (2.0 * kind - 1.0) * (0.1 + timesteps[group].astype(jnp.float32) / 1000.0) / (counts.astype(jnp.float32) * TPF)
        slot_hot = (tag[:, None] == jnp.arange(CLIPS).astype(jnp.int32)[None, :]).astype(jnp.float32)
        slot_coef = lax.optimization_barrier(jnp.sum(slot_hot * coef[None, :], axis=1))
        slot_kind = lax.optimization_barrier(jnp.sum(slot_hot * kind[None, :], axis=1))
        states = hidden[group].astype(jnp.float32)
        mean = lax.optimization_barrier(jnp.mean(states, axis=1, keepdims=True))
        centred = states - mean
        var = lax.optimization_barrier(jnp.mean(centred * centred, axis=1, keepdims=True))
        normed = (centred * lax.rsqrt(var + 1e-06)).astype(jnp.bfloat16)
        pred = jnp.dot(normed, w_out, preferred_element_type=jnp.float32)
        target = slot_kind[:, None] * teacher[group] + (1.0 - slot_kind[:, None]) * (noise[group] - x0)
        diff = pred - target
        err = lax.optimization_barrier(jnp.sum(diff * diff, axis=1))
        losses.append(coef * lax.optimization_barrier(jnp.sum(slot_hot * err[:, None], axis=0)))
        dpred = (2.0 * slot_coef[:, None] * diff).astype(jnp.bfloat16)
        grad_out = grad_out + jnp.dot(normed.T, dpred, preferred_element_type=jnp.float32)
    return (jnp.stack(latents), jnp.stack(losses), grad_out)
```

```python
import jax
import jax.numpy as jnp
from jax import lax
from jax.sharding import PartitionSpec as P

LAT = 64
CLIPS = 4


def with_halo(cells, sides, width):
    for axis, dim in sides:
        count = lax.axis_size(axis)
        ends = count - 1
        head = lax.slice_in_dim(cells, 0, width, axis=dim)
        tail = lax.slice_in_dim(cells, cells.shape[dim] - width, cells.shape[dim], axis=dim)
        cells = jnp.concatenate(
            [
                lax.ppermute(tail, axis, [(i, (i + 1) % count) for i in range(ends)]),
                cells,
                lax.ppermute(head, axis, [((i + 1) % count, i) for i in range(ends)]),
            ],
            axis=dim,
        )
    return cells


def tree_reduce(grad_part, loss_row, nseq, ndp):
    rows = grad_part.shape[0] // nseq
    nbits = nseq.bit_length() - 1
    assert 1 << nbits == nseq and ndp & (ndp - 1) == 0
    blocks = grad_part.reshape(nseq, rows, LAT)
    extra = jnp.broadcast_to(loss_row[None, None, :], (nseq, 1, LAT))
    x = jnp.concatenate([blocks, extra], axis=1).reshape((2,) * nbits + (rows + 1, LAT))
    me = lax.axis_index("seq")
    left = list(range(nbits - 1, -1, -1))
    for k in range(nbits):
        axis = left.index(k)
        bit = (me >> k) & 1
        keep = lax.dynamic_index_in_dim(x, bit, axis, keepdims=False)
        send = lax.dynamic_index_in_dim(x, 1 - bit, axis, keepdims=False)
        x = keep + lax.ppermute(send, "seq", [(i, i ^ (1 << k)) for i in range(nseq)])
        left.pop(axis)
    x = x.reshape(rows + 1, LAT)
    for k in range(ndp.bit_length() - 1):
        x = x + lax.ppermute(x, "dp", [(i, i ^ (1 << k)) for i in range(ndp)])
    return x


def conv_rows(padded, kernel, keep, first, count):
    nframes = keep.shape[1]
    width = padded.shape[2] - 2
    chans = padded.shape[3]
    total = jnp.zeros((nframes, count * width, chans), jnp.float32)
    for lag in range(3):
        pieces = [
            padded[2 - lag : 2 - lag + nframes, first + i : first + i + count, j : j + width, :]
            for i in range(3)
            for j in range(3)
        ]
        columns = jnp.concatenate(pieces, axis=-1).reshape(-1, 9 * chans)
        part = jnp.dot(
            columns, kernel[lag].reshape(9 * chans, chans), preferred_element_type=jnp.float32
        )
        total = total + part.reshape(nframes, count * width, chans) * keep[lag][:, None, None]
    return total.reshape(nframes, count, width, chans)


def per_device(
    frames,
    frame_counts,
    clip_group,
    timesteps,
    owner_map,
    conv_weight,
    w_latent,
    hidden,
    noise,
    teacher,
    w_out,
):
    nseq = lax.axis_size("seq")
    local = frames[0]
    nframes, nrows, width, chans = local.shape
    tok_rows = nrows // 4
    tok_cols = width // 4
    per_frame = nrows * nseq // 4 * tok_cols
    counts = frame_counts[0]
    ends = jnp.cumsum(counts)
    index = jnp.arange(nframes, dtype=jnp.int32)
    clip_of = jnp.sum((index[:, None] >= ends[None, :]).astype(jnp.int32), axis=1)
    clip_hot = (clip_of[:, None] == jnp.arange(CLIPS, dtype=jnp.int32)[None, :]).astype(jnp.int32)
    starts = jnp.sum(clip_hot * (ends - counts)[None, :], axis=1)
    keep = jnp.stack([(index - lag >= starts).astype(jnp.float32) for lag in range(3)])
    rimmed = with_halo(frames, (("seq", 2),), 1)[0]
    outer_pad = jnp.pad(rimmed, ((2, 0), (0, 0), (1, 1), (0, 0)))
    conv = conv_rows(outer_pad, conv_weight, keep, 0, nrows)
    cells = (local.astype(jnp.float32) + jax.nn.silu(conv)).astype(jnp.bfloat16)
    patches = (
        cells.reshape(nframes, tok_rows, 4, tok_cols, 4, chans)
        .transpose(0, 1, 3, 2, 4, 5)
        .reshape(-1, 16 * chans)
    )
    tokens = jnp.dot(patches, w_latent, preferred_element_type=jnp.float32).astype(jnp.bfloat16)
    latent_out = tokens.reshape(1, nframes, tok_rows, tok_cols * LAT)
    slots = hidden.shape[1]
    capacity = slots // nseq
    owners = owner_map.reshape(-1)
    owner_hot = (owners[:, None] == jnp.arange(nseq, dtype=jnp.int32)[None, :]).astype(jnp.int32)
    rank = jnp.sum(jnp.cumsum(owner_hot, axis=0) * owner_hot, axis=1) - 1
    dest = owners * capacity + rank
    select = (dest[None, :] == jnp.arange(slots, dtype=jnp.int32)[:, None]).astype(jnp.bfloat16)
    tok_clip = jnp.repeat(clip_of, tok_rows * tok_cols).astype(jnp.float32) + 1.0
    outgoing = (
        jnp.dot(select, tokens, preferred_element_type=jnp.float32)
        .astype(jnp.bfloat16)
        .reshape(nseq, capacity, LAT)
    )
    labels = (
        jnp.dot(select, tok_clip.astype(jnp.bfloat16)[:, None], preferred_element_type=jnp.float32)
        .astype(jnp.bfloat16)
        .reshape(nseq, capacity)
    )
    arrived, arrived_tags = (
        lax.all_to_all(outgoing, "seq", split_axis=0, concat_axis=0, tiled=True),
        lax.all_to_all(labels, "seq", split_axis=0, concat_axis=0, tiled=True),
    )
    x0 = arrived.reshape(slots, LAT).astype(jnp.float32)
    tag = arrived_tags.reshape(slots).astype(jnp.float32)
    kind = clip_group[0].astype(jnp.float32)
    coef = (
        (2.0 * kind - 1.0)
        * (0.1 + timesteps[0].astype(jnp.float32) / 1000.0)
        / (counts.astype(jnp.float32) * per_frame)
    )
    slot_hot = (tag[:, None] == (jnp.arange(CLIPS, dtype=jnp.float32) + 1.0)[None, :]).astype(
        jnp.float32
    )
    slot_coef = jnp.sum(slot_hot * coef[None, :], axis=1)
    slot_kind = jnp.sum(slot_hot * kind[None, :], axis=1)
    states = hidden[0].astype(jnp.float32)
    mean = jnp.mean(states, axis=1, keepdims=True)
    centred = states - mean
    var = jnp.mean(centred * centred, axis=1, keepdims=True)
    normed = (centred * lax.rsqrt(var + 1e-06)).astype(jnp.bfloat16)
    pred = jnp.dot(normed, w_out, preferred_element_type=jnp.float32)
    target = slot_kind[:, None] * teacher[0] + (1.0 - slot_kind[:, None]) * (noise[0] - x0)
    diff = pred - target
    err = jnp.sum(diff * diff, axis=1)
    partial_loss = coef * jnp.sum(slot_hot * err[:, None], axis=0)
    dpred = (2.0 * slot_coef[:, None] * diff).astype(jnp.bfloat16)
    grad_part = lax.dot_general(
        normed, dpred, (((0,), (0,)), ((), ())), preferred_element_type=jnp.float32
    )
    ndp = lax.axis_size("dp")
    place = lax.axis_index("dp") * CLIPS
    loss_row = lax.dynamic_update_slice(jnp.zeros((LAT,), jnp.float32), partial_loss, (place,))
    summed = tree_reduce(grad_part, loss_row, nseq, ndp)
    grad_mine = summed[:-1]
    clip_loss = lax.dynamic_slice_in_dim(summed[-1], place, CLIPS).reshape(1, CLIPS)
    return (latent_out, clip_loss, grad_mine)


def solution(mesh):
    return jax.shard_map(
        per_device,
        mesh=mesh,
        in_specs=(
            P("dp", None, "seq", None, None),
            P("dp", None),
            P("dp", None),
            P("dp", None),
            P("dp", "seq", None, None),
            P(),
            P(),
            P("dp", "seq", None),
            P("dp", "seq", None),
            P("dp", "seq", None),
            P(),
        ),
        out_specs=(P("dp", None, "seq", None), P("dp", None), P("seq", None)),
        check_vma=False,
    )
```

```python
import jax
import jax.numpy as jnp
from jax import lax
from jax.sharding import PartitionSpec as P

LAT = 64
CLIPS = 4


def with_halo(cells, sides, width):
    for axis, dim in sides:
        count = lax.axis_size(axis)
        ends = count - 1
        head = lax.slice_in_dim(cells, 0, width, axis=dim)
        tail = lax.slice_in_dim(cells, cells.shape[dim] - width, cells.shape[dim], axis=dim)
        cells = jnp.concatenate(
            [
                lax.ppermute(tail, axis, [(i, (i + 1) % count) for i in range(ends)]),
                cells,
                lax.ppermute(head, axis, [((i + 1) % count, i) for i in range(ends)]),
            ],
            axis=dim,
        )
    return cells


def causal_conv(rimmed, conv_weight, keep):
    nframes = rimmed.shape[0]
    chans = rimmed.shape[-1]
    padded = jnp.pad(rimmed, ((0, 0), (0, 0), (1, 1), (0, 0)))
    kernel = jnp.transpose(conv_weight, (1, 2, 3, 0, 4)).reshape(3, 3, chans, 3 * chans)
    each = lax.conv_general_dilated(
        padded,
        kernel,
        (1, 1),
        "VALID",
        dimension_numbers=("NHWC", "HWIO", "NHWC"),
        preferred_element_type=jnp.float32,
    )
    total = each[..., :chans]
    for lag in (1, 2):
        part = each[: nframes - lag, ..., lag * chans : (lag + 1) * chans]
        part = jnp.pad(part, ((lag, 0), (0, 0), (0, 0), (0, 0)))
        total = total + part * keep[lag][:, None, None, None]
    return total


def tree_reduce(grad_t, loss_line, nseq, ndp):
    rows = grad_t.shape[1] // nseq
    nbits = nseq.bit_length() - 1
    assert 1 << nbits == nseq and ndp & (ndp - 1) == 0
    x = jnp.concatenate([grad_t, loss_line[None, :]], axis=0)
    x = x.reshape((x.shape[0],) + (2,) * nbits + (rows,))
    me = lax.axis_index("seq")
    left = list(range(nbits - 1, -1, -1))
    for k in range(nbits):
        axis = left.index(k) + 1
        bit = (me >> k) & 1
        keep = lax.dynamic_index_in_dim(x, bit, axis, keepdims=False)
        send = lax.dynamic_index_in_dim(x, 1 - bit, axis, keepdims=False)
        x = keep + lax.ppermute(send, "seq", [(i, i ^ (1 << k)) for i in range(nseq)])
        left.pop(axis - 1)
    x = x.reshape(-1, rows)
    for k in range(ndp.bit_length() - 1):
        x = x + lax.ppermute(x, "dp", [(i, i ^ (1 << k)) for i in range(ndp)])
    return x


def per_device(
    frames,
    frame_counts,
    clip_group,
    timesteps,
    owner_map,
    conv_weight,
    w_latent,
    hidden,
    noise,
    teacher,
    w_out,
):
    nseq = lax.axis_size("seq")
    local = frames[0]
    nframes, nrows, width, chans = local.shape
    tok_rows = nrows // 4
    tok_cols = width // 4
    per_frame = nrows * nseq // 4 * tok_cols
    counts = frame_counts[0]
    ends = jnp.cumsum(counts)
    index = jnp.arange(nframes, dtype=jnp.int32)
    clip_of = jnp.sum((index[:, None] >= ends[None, :]).astype(jnp.int32), axis=1)
    clip_hot = (clip_of[:, None] == jnp.arange(CLIPS, dtype=jnp.int32)[None, :]).astype(jnp.int32)
    starts = jnp.sum(clip_hot * (ends - counts)[None, :], axis=1)
    keep = jnp.stack([(index - lag >= starts).astype(jnp.float32) for lag in range(3)])
    rimmed = with_halo(frames, (("seq", 2),), 1)[0]
    conv = causal_conv(rimmed, conv_weight, keep)
    cells = (local.astype(jnp.float32) + jax.nn.silu(conv)).astype(jnp.bfloat16)
    tokens = lax.conv_general_dilated(
        cells,
        w_latent.reshape(4, 4, chans, LAT),
        (4, 4),
        "VALID",
        dimension_numbers=("NHWC", "HWIO", "NHWC"),
        preferred_element_type=jnp.float32,
    ).astype(jnp.bfloat16)
    latent_out = tokens.reshape(1, nframes, tok_rows, tok_cols * LAT)
    tokens = tokens.reshape(-1, LAT)
    slots = hidden.shape[1]
    capacity = slots // nseq
    assert capacity <= LAT
    owners = owner_map.reshape(-1)
    owner_hot = (owners[:, None] == jnp.arange(nseq, dtype=jnp.int32)[None, :]).astype(jnp.int32)
    rank = jnp.sum(jnp.cumsum(owner_hot, axis=0) * owner_hot, axis=1) - 1
    dest = owners * capacity + rank
    select = (dest[None, :] == jnp.arange(slots, dtype=jnp.int32)[:, None]).astype(jnp.bfloat16)
    tok_clip = jnp.repeat(clip_of, tok_rows * tok_cols).astype(jnp.float32) + 1.0
    outgoing = (
        jnp.dot(select, tokens, preferred_element_type=jnp.float32)
        .astype(jnp.bfloat16)
        .reshape(nseq, capacity, LAT)
    )
    labels = (
        jnp.dot(select, tok_clip.astype(jnp.bfloat16)[:, None], preferred_element_type=jnp.float32)
        .astype(jnp.bfloat16)
        .reshape(nseq, 1, capacity)
    )
    labels = jnp.pad(labels, ((0, 0), (0, 0), (0, LAT - capacity)))
    arrived = lax.all_to_all(
        jnp.concatenate([outgoing, labels], axis=1), "seq", split_axis=0, concat_axis=0, tiled=True
    )
    x0 = arrived[:, :capacity].reshape(slots, LAT).astype(jnp.float32)
    tag = arrived[:, capacity, :capacity].reshape(slots).astype(jnp.float32)
    kind = clip_group[0].astype(jnp.float32)
    coef = (
        (2.0 * kind - 1.0)
        * (0.1 + timesteps[0].astype(jnp.float32) / 1000.0)
        / (counts.astype(jnp.float32) * per_frame)
    )
    slot_hot = (tag[:, None] == (jnp.arange(CLIPS, dtype=jnp.float32) + 1.0)[None, :]).astype(
        jnp.float32
    )
    slot_coef = jnp.sum(slot_hot * coef[None, :], axis=1)
    slot_kind = jnp.sum(slot_hot * kind[None, :], axis=1)
    states = hidden[0].astype(jnp.float32)
    mean = jnp.mean(states, axis=1, keepdims=True)
    centred = states - mean
    var = jnp.mean(centred * centred, axis=1, keepdims=True)
    normed = (centred * lax.rsqrt(var + 1e-06)).astype(jnp.bfloat16)
    pred = jnp.dot(normed, w_out, preferred_element_type=jnp.float32)
    target = slot_kind[:, None] * teacher[0] + (1.0 - slot_kind[:, None]) * (noise[0] - x0)
    diff = pred - target
    err = jnp.sum(diff * diff, axis=1)
    partial_loss = coef * jnp.sum(slot_hot * err[:, None], axis=0)
    dpred = (2.0 * slot_coef[:, None] * diff).astype(jnp.bfloat16)
    grad_t = lax.dot_general(
        dpred, normed, (((0,), (0,)), ((), ())), preferred_element_type=jnp.float32
    )
    ndp = lax.axis_size("dp")
    share = grad_t.shape[1] // nseq
    assert ndp * CLIPS <= share
    place = lax.axis_index("dp") * CLIPS
    loss_row = lax.dynamic_update_slice(jnp.zeros((share,), jnp.float32), partial_loss, (place,))
    summed = tree_reduce(grad_t, jnp.tile(loss_row, nseq), nseq, ndp)
    grad_mine = summed[:LAT].T
    clip_loss = lax.dynamic_slice_in_dim(summed[LAT], place, CLIPS).reshape(1, CLIPS)
    return (latent_out, clip_loss, grad_mine)


def solution(mesh):
    return jax.shard_map(
        per_device,
        mesh=mesh,
        in_specs=(
            P("dp", None, "seq", None, None),
            P("dp", None),
            P("dp", None),
            P("dp", None),
            P("dp", "seq", None, None),
            P(),
            P(),
            P("dp", "seq", None),
            P("dp", "seq", None),
            P("dp", "seq", None),
            P(),
        ),
        out_specs=(P("dp", None, "seq", None), P("dp", None), P("seq", None)),
        check_vma=False,
    )
```

```python
import jax
import jax.numpy as jnp
from jax import lax
from jax.experimental import pallas as pl
from jax.experimental.pallas import tpu as pltpu
from jax.sharding import PartitionSpec as P

LAT = 64
CLIPS = 4


def with_halo(cells, sides, width):
    for axis, dim in sides:
        count = lax.axis_size(axis)
        ends = count - 1
        head = lax.slice_in_dim(cells, 0, width, axis=dim)
        tail = lax.slice_in_dim(cells, cells.shape[dim] - width, cells.shape[dim], axis=dim)
        cells = jnp.concatenate(
            [
                lax.ppermute(tail, axis, [(i, (i + 1) % count) for i in range(ends)]),
                cells,
                lax.ppermute(head, axis, [((i + 1) % count, i) for i in range(ends)]),
            ],
            axis=dim,
        )
    return cells


def causal_conv(rimmed, conv_weight, keep):
    nframes = rimmed.shape[0]
    padded = jnp.pad(rimmed, ((0, 0), (0, 0), (1, 1), (0, 0)))
    total = None
    for lag in range(3):
        part = lax.conv_general_dilated(
            padded[: nframes - lag],
            conv_weight[lag],
            (1, 1),
            "VALID",
            dimension_numbers=("NHWC", "HWIO", "NHWC"),
            preferred_element_type=jnp.float32,
        )
        if lag == 0:
            total = part
        else:
            part = jnp.pad(part, ((lag, 0), (0, 0), (0, 0), (0, 0)))
            total = total + part * keep[lag][:, None, None, None]
    return total


def _grad_kernel(dpt_ref, normed_ref, out_ref):
    out_ref[...] = jnp.dot(dpt_ref[...], normed_ref[...], preferred_element_type=jnp.float32)


def grad_matmul(dpt, normed):
    lat, slots = dpt.shape
    feats = normed.shape[1]
    tile = 512 if feats % 512 == 0 else feats
    return pl.pallas_call(
        _grad_kernel,
        out_shape=jax.ShapeDtypeStruct((lat, feats), jnp.float32),
        grid=(feats // tile,),
        in_specs=[
            pl.BlockSpec((lat, slots), lambda i: (0, 0)),
            pl.BlockSpec((slots, tile), lambda i: (0, i)),
        ],
        out_specs=pl.BlockSpec((lat, tile), lambda i: (0, i)),
        cost_estimate=pl.CostEstimate(
            flops=2 * lat * slots * feats,
            bytes_accessed=2 * lat * slots + 2 * slots * feats + 4 * lat * feats,
            transcendentals=0,
        ),
    )(dpt, normed)


def tree_reduce(grad_t, loss_line, nseq, ndp):
    rows = grad_t.shape[1] // nseq
    nbits = nseq.bit_length() - 1
    assert 1 << nbits == nseq and ndp & (ndp - 1) == 0
    x = jnp.concatenate([grad_t, loss_line[None, :]], axis=0)
    x = x.reshape((x.shape[0],) + (2,) * nbits + (rows,))
    me = lax.axis_index("seq")
    left = list(range(nbits - 1, -1, -1))
    for k in range(nbits):
        axis = left.index(k) + 1
        bit = (me >> k) & 1
        keep = lax.dynamic_index_in_dim(x, bit, axis, keepdims=False)
        send = lax.dynamic_index_in_dim(x, 1 - bit, axis, keepdims=False)
        x = keep + lax.ppermute(send, "seq", [(i, i ^ (1 << k)) for i in range(nseq)])
        left.pop(axis - 1)
    x = x.reshape(-1, rows)
    for k in range(ndp.bit_length() - 1):
        x = x + lax.ppermute(x, "dp", [(i, i ^ (1 << k)) for i in range(ndp)])
    return x


def per_device(
    frames,
    frame_counts,
    clip_group,
    timesteps,
    owner_map,
    conv_weight,
    w_latent,
    hidden,
    noise,
    teacher,
    w_out,
):
    nseq = lax.axis_size("seq")
    local = frames[0]
    nframes, nrows, width, chans = local.shape
    tok_rows = nrows // 4
    tok_cols = width // 4
    per_frame = nrows * nseq // 4 * tok_cols
    counts = frame_counts[0]
    ends = jnp.cumsum(counts)
    index = jnp.arange(nframes, dtype=jnp.int32)
    clip_of = jnp.sum((index[:, None] >= ends[None, :]).astype(jnp.int32), axis=1)
    clip_hot = (clip_of[:, None] == jnp.arange(CLIPS, dtype=jnp.int32)[None, :]).astype(jnp.int32)
    starts = jnp.sum(clip_hot * (ends - counts)[None, :], axis=1)
    keep = jnp.stack([(index - lag >= starts).astype(jnp.float32) for lag in range(3)])
    rimmed = with_halo(frames, (("seq", 2),), 1)[0]
    conv = causal_conv(rimmed, conv_weight, keep)
    cells = (local.astype(jnp.float32) + jax.nn.silu(conv)).astype(jnp.bfloat16)
    tokens = lax.conv_general_dilated(
        cells,
        w_latent.reshape(4, 4, chans, LAT),
        (4, 4),
        "VALID",
        dimension_numbers=("NHWC", "HWIO", "NHWC"),
        preferred_element_type=jnp.float32,
    ).astype(jnp.bfloat16)
    latent_out = tokens.reshape(1, nframes, tok_rows, tok_cols * LAT)
    tokens = tokens.reshape(-1, LAT)
    slots = hidden.shape[1]
    capacity = slots // nseq
    assert capacity <= LAT
    owners = owner_map.reshape(-1)
    owner_hot = (owners[:, None] == jnp.arange(nseq, dtype=jnp.int32)[None, :]).astype(jnp.int32)
    rank = jnp.sum(jnp.cumsum(owner_hot, axis=0) * owner_hot, axis=1) - 1
    dest = owners * capacity + rank
    select = (dest[None, :] == jnp.arange(slots, dtype=jnp.int32)[:, None]).astype(jnp.bfloat16)
    tok_clip = jnp.repeat(clip_of, tok_rows * tok_cols).astype(jnp.float32) + 1.0
    outgoing = (
        jnp.dot(select, tokens, preferred_element_type=jnp.float32)
        .astype(jnp.bfloat16)
        .reshape(nseq, capacity, LAT)
    )
    labels = (
        jnp.dot(select, tok_clip.astype(jnp.bfloat16)[:, None], preferred_element_type=jnp.float32)
        .astype(jnp.bfloat16)
        .reshape(nseq, 1, capacity)
    )
    labels = jnp.pad(labels, ((0, 0), (0, 0), (0, LAT - capacity)))
    arrived = lax.all_to_all(
        jnp.concatenate([outgoing, labels], axis=1), "seq", split_axis=0, concat_axis=0, tiled=True
    )
    x0 = arrived[:, :capacity].reshape(slots, LAT).astype(jnp.float32)
    tag = arrived[:, capacity, :capacity].reshape(slots).astype(jnp.float32)
    kind = clip_group[0].astype(jnp.float32)
    coef = (
        (2.0 * kind - 1.0)
        * (0.1 + timesteps[0].astype(jnp.float32) / 1000.0)
        / (counts.astype(jnp.float32) * per_frame)
    )
    slot_hot = (tag[:, None] == (jnp.arange(CLIPS, dtype=jnp.float32) + 1.0)[None, :]).astype(
        jnp.float32
    )
    slot_coef = jnp.sum(slot_hot * coef[None, :], axis=1)
    slot_kind = jnp.sum(slot_hot * kind[None, :], axis=1)
    states = hidden[0].astype(jnp.float32)
    mean = jnp.mean(states, axis=1, keepdims=True)
    centred = states - mean
    var = jnp.mean(centred * centred, axis=1, keepdims=True)
    normed = (centred * lax.rsqrt(var + 1e-06)).astype(jnp.bfloat16)
    pred = jnp.dot(normed, w_out, preferred_element_type=jnp.float32)
    target = slot_kind[:, None] * teacher[0] + (1.0 - slot_kind[:, None]) * (noise[0] - x0)
    diff = pred - target
    err = jnp.sum(diff * diff, axis=1)
    partial_loss = coef * jnp.sum(slot_hot * err[:, None], axis=0)
    dpred = (2.0 * slot_coef[:, None] * diff).astype(jnp.bfloat16)
    grad_t = grad_matmul(dpred.T, normed)
    ndp = lax.axis_size("dp")
    share = grad_t.shape[1] // nseq
    assert ndp * CLIPS <= share
    place = lax.axis_index("dp") * CLIPS
    loss_row = lax.dynamic_update_slice(jnp.zeros((share,), jnp.float32), partial_loss, (place,))
    summed = tree_reduce(grad_t, jnp.tile(loss_row, nseq), nseq, ndp)
    grad_mine = summed[:LAT].T
    clip_loss = lax.dynamic_slice_in_dim(summed[LAT], place, CLIPS).reshape(1, CLIPS)
    return (latent_out, clip_loss, grad_mine)


def solution(mesh):
    return jax.shard_map(
        per_device,
        mesh=mesh,
        in_specs=(
            P("dp", None, "seq", None, None),
            P("dp", None),
            P("dp", None),
            P("dp", None),
            P("dp", "seq", None, None),
            P(),
            P(),
            P("dp", "seq", None),
            P("dp", "seq", None),
            P("dp", "seq", None),
            P(),
        ),
        out_specs=(P("dp", None, "seq", None), P("dp", None), P("seq", None)),
        check_vma=False,
    )
```

```python
import jax
import jax.numpy as jnp
from jax import lax
from jax.experimental import pallas as pl
from jax.sharding import PartitionSpec as P

LAT = 64
CLIPS = 4


def with_halo(cells, sides, width):
    for axis, dim in sides:
        count = lax.axis_size(axis)
        ends = count - 1
        head = lax.slice_in_dim(cells, 0, width, axis=dim)
        tail = lax.slice_in_dim(cells, cells.shape[dim] - width, cells.shape[dim], axis=dim)
        cells = jnp.concatenate(
            [
                lax.ppermute(tail, axis, [(i, (i + 1) % count) for i in range(ends)]),
                cells,
                lax.ppermute(head, axis, [((i + 1) % count, i) for i in range(ends)]),
            ],
            axis=dim,
        )
    return cells


def causal_conv(rimmed, conv_weight, keep):
    nframes = rimmed.shape[0]
    chans = rimmed.shape[-1]
    padded = jnp.pad(rimmed, ((0, 0), (0, 0), (1, 1), (0, 0)))
    kernel = jnp.transpose(conv_weight, (1, 2, 3, 0, 4)).reshape(3, 3, chans, 3 * chans)
    each = lax.conv_general_dilated(
        padded,
        kernel,
        (1, 1),
        "VALID",
        dimension_numbers=("NHWC", "HWIO", "NHWC"),
        preferred_element_type=jnp.float32,
    )
    total = each[..., :chans]
    for lag in (1, 2):
        part = each[: nframes - lag, ..., lag * chans : (lag + 1) * chans]
        part = jnp.pad(part, ((lag, 0), (0, 0), (0, 0), (0, 0)))
        total = total + part * keep[lag][:, None, None, None]
    return total


def _grad_kernel(normed_ref, dpred_ref, out_ref):
    out_ref[...] = lax.dot_general(
        normed_ref[...], dpred_ref[...], (((0,), (0,)), ((), ())), preferred_element_type=jnp.float32
    )


def grad_matmul(normed, dpred):
    slots, feats = normed.shape
    lat = dpred.shape[1]
    tile = 512 if feats % 512 == 0 else feats
    return pl.pallas_call(
        _grad_kernel,
        out_shape=jax.ShapeDtypeStruct((feats, lat), jnp.float32),
        grid=(feats // tile,),
        in_specs=[
            pl.BlockSpec((slots, tile), lambda i: (0, i)),
            pl.BlockSpec((slots, lat), lambda i: (0, 0)),
        ],
        out_specs=pl.BlockSpec((tile, lat), lambda i: (i, 0)),
        cost_estimate=pl.CostEstimate(
            flops=2 * lat * slots * feats,
            bytes_accessed=2 * lat * slots + 2 * slots * feats + 4 * lat * feats,
            transcendentals=0,
        ),
    )(normed, dpred)


def tree_reduce(grad_part, loss_row, nseq, ndp):
    rows = grad_part.shape[0] // nseq
    nbits = nseq.bit_length() - 1
    assert 1 << nbits == nseq and ndp & (ndp - 1) == 0
    blocks = grad_part.reshape(nseq, rows, LAT)
    extra = jnp.broadcast_to(loss_row[None, None, :], (nseq, 1, LAT))
    x = jnp.concatenate([blocks, extra], axis=1).reshape((2,) * nbits + (rows + 1, LAT))
    me = lax.axis_index("seq")
    left = list(range(nbits - 1, -1, -1))
    for k in range(nbits):
        axis = left.index(k)
        bit = (me >> k) & 1
        keep = lax.dynamic_index_in_dim(x, bit, axis, keepdims=False)
        send = lax.dynamic_index_in_dim(x, 1 - bit, axis, keepdims=False)
        x = keep + lax.ppermute(send, "seq", [(i, i ^ (1 << k)) for i in range(nseq)])
        left.pop(axis)
    x = x.reshape(rows + 1, LAT)
    for k in range(ndp.bit_length() - 1):
        x = x + lax.ppermute(x, "dp", [(i, i ^ (1 << k)) for i in range(ndp)])
    return x


def per_device(
    frames,
    frame_counts,
    clip_group,
    timesteps,
    owner_map,
    conv_weight,
    w_latent,
    hidden,
    noise,
    teacher,
    w_out,
):
    nseq = lax.axis_size("seq")
    local = frames[0]
    nframes, nrows, width, chans = local.shape
    tok_rows = nrows // 4
    tok_cols = width // 4
    per_frame = nrows * nseq // 4 * tok_cols
    counts = frame_counts[0]
    ends = jnp.cumsum(counts)
    index = jnp.arange(nframes, dtype=jnp.int32)
    clip_of = jnp.sum((index[:, None] >= ends[None, :]).astype(jnp.int32), axis=1)
    clip_hot = (clip_of[:, None] == jnp.arange(CLIPS, dtype=jnp.int32)[None, :]).astype(jnp.int32)
    starts = jnp.sum(clip_hot * (ends - counts)[None, :], axis=1)
    keep = jnp.stack([(index - lag >= starts).astype(jnp.float32) for lag in range(3)])
    rimmed = with_halo(frames, (("seq", 2),), 1)[0]
    conv = causal_conv(rimmed, conv_weight, keep)
    cells = (local.astype(jnp.float32) + jax.nn.silu(conv)).astype(jnp.bfloat16)
    tokens = lax.conv_general_dilated(
        cells,
        w_latent.reshape(4, 4, chans, LAT),
        (4, 4),
        "VALID",
        dimension_numbers=("NHWC", "HWIO", "NHWC"),
        preferred_element_type=jnp.float32,
    ).astype(jnp.bfloat16)
    latent_out = tokens.reshape(1, nframes, tok_rows, tok_cols * LAT)
    tokens = tokens.reshape(-1, LAT)
    slots = hidden.shape[1]
    capacity = slots // nseq
    assert capacity <= LAT
    owners = owner_map.reshape(-1)
    owner_hot = (owners[:, None] == jnp.arange(nseq, dtype=jnp.int32)[None, :]).astype(jnp.int32)
    rank = jnp.sum(jnp.cumsum(owner_hot, axis=0) * owner_hot, axis=1) - 1
    dest = owners * capacity + rank
    select = (dest[None, :] == jnp.arange(slots, dtype=jnp.int32)[:, None]).astype(jnp.bfloat16)
    tok_clip = jnp.repeat(clip_of, tok_rows * tok_cols).astype(jnp.float32) + 1.0
    outgoing = (
        jnp.dot(select, tokens, preferred_element_type=jnp.float32)
        .astype(jnp.bfloat16)
        .reshape(nseq, capacity, LAT)
    )
    labels = (
        jnp.dot(select, tok_clip.astype(jnp.bfloat16)[:, None], preferred_element_type=jnp.float32)
        .astype(jnp.bfloat16)
        .reshape(nseq, 1, capacity)
    )
    labels = jnp.pad(labels, ((0, 0), (0, 0), (0, LAT - capacity)))
    arrived = lax.all_to_all(
        jnp.concatenate([outgoing, labels], axis=1), "seq", split_axis=0, concat_axis=0, tiled=True
    )
    x0 = arrived[:, :capacity].reshape(slots, LAT).astype(jnp.float32)
    tag = arrived[:, capacity, :capacity].reshape(slots).astype(jnp.float32)
    kind = clip_group[0].astype(jnp.float32)
    coef = (
        (2.0 * kind - 1.0)
        * (0.1 + timesteps[0].astype(jnp.float32) / 1000.0)
        / (counts.astype(jnp.float32) * per_frame)
    )
    slot_hot = (tag[:, None] == (jnp.arange(CLIPS, dtype=jnp.float32) + 1.0)[None, :]).astype(
        jnp.float32
    )
    slot_coef = jnp.sum(slot_hot * coef[None, :], axis=1)
    slot_kind = jnp.sum(slot_hot * kind[None, :], axis=1)
    states = hidden[0].astype(jnp.float32)
    mean = jnp.mean(states, axis=1, keepdims=True)
    centred = states - mean
    var = jnp.mean(centred * centred, axis=1, keepdims=True)
    normed = (centred * lax.rsqrt(var + 1e-06)).astype(jnp.bfloat16)
    pred = jnp.dot(normed, w_out, preferred_element_type=jnp.float32)
    target = slot_kind[:, None] * teacher[0] + (1.0 - slot_kind[:, None]) * (noise[0] - x0)
    diff = pred - target
    err = jnp.sum(diff * diff, axis=1)
    partial_loss = coef * jnp.sum(slot_hot * err[:, None], axis=0)
    dpred = (2.0 * slot_coef[:, None] * diff).astype(jnp.bfloat16)
    grad_part = grad_matmul(normed, dpred)
    ndp = lax.axis_size("dp")
    assert ndp * CLIPS <= LAT
    place = lax.axis_index("dp") * CLIPS
    loss_row = lax.dynamic_update_slice(jnp.zeros((LAT,), jnp.float32), partial_loss, (place,))
    summed = tree_reduce(grad_part, loss_row, nseq, ndp)
    grad_mine = summed[:-1]
    clip_loss = lax.dynamic_slice_in_dim(summed[-1], place, CLIPS).reshape(1, CLIPS)
    return (latent_out, clip_loss, grad_mine)


def solution(mesh):
    return jax.shard_map(
        per_device,
        mesh=mesh,
        in_specs=(
            P("dp", None, "seq", None, None),
            P("dp", None),
            P("dp", None),
            P("dp", None),
            P("dp", "seq", None, None),
            P(),
            P(),
            P("dp", "seq", None),
            P("dp", "seq", None),
            P("dp", "seq", None),
            P(),
        ),
        out_specs=(P("dp", None, "seq", None), P("dp", None), P("seq", None)),
        check_vma=False,
    )
```

```python
import jax
import jax.numpy as jnp
from jax import lax
from jax.sharding import PartitionSpec as P

LAT = 64
CLIPS = 4


def with_halo(cells, sides, width):
    for axis, dim in sides:
        count = lax.axis_size(axis)
        ends = count - 1
        head = lax.slice_in_dim(cells, 0, width, axis=dim)
        tail = lax.slice_in_dim(cells, cells.shape[dim] - width, cells.shape[dim], axis=dim)
        cells = jnp.concatenate(
            [
                lax.ppermute(tail, axis, [(i, (i + 1) % count) for i in range(ends)]),
                cells,
                lax.ppermute(head, axis, [((i + 1) % count, i) for i in range(ends)]),
            ],
            axis=dim,
        )
    return cells


def causal_conv(rimmed, conv_weight, keep):
    nframes = rimmed.shape[0]
    chans = rimmed.shape[-1]
    padded = jnp.pad(rimmed, ((0, 0), (0, 0), (1, 1), (0, 0)))
    kernel = jnp.transpose(conv_weight, (1, 2, 3, 0, 4)).reshape(3, 3, chans, 3 * chans)
    each = lax.conv_general_dilated(
        padded,
        kernel,
        (1, 1),
        "VALID",
        dimension_numbers=("NHWC", "HWIO", "NHWC"),
        preferred_element_type=jnp.float32,
    )
    total = each[..., :chans]
    for lag in (1, 2):
        part = each[: nframes - lag, ..., lag * chans : (lag + 1) * chans]
        part = jnp.pad(part, ((lag, 0), (0, 0), (0, 0), (0, 0)))
        total = total + part * keep[lag][:, None, None, None]
    return total


def tree_reduce(grad_t, loss_line, nseq, ndp):
    rows = grad_t.shape[1] // nseq
    nbits = nseq.bit_length() - 1
    assert 1 << nbits == nseq and ndp & (ndp - 1) == 0
    groups = [1, 2] + [1] * (nbits - 3) if nbits >= 3 else [1] * nbits
    x = jnp.concatenate([grad_t, loss_line[None, :]], axis=0)
    x = x.reshape(x.shape[0], nseq, rows)
    me = lax.axis_index("seq")
    low = 0
    for width in groups:
        ways = 1 << width
        x = x.reshape(x.shape[0], x.shape[1] // ways, ways, rows)
        digit = (me >> low) & (ways - 1)
        total = lax.dynamic_index_in_dim(x, digit, 2, keepdims=False)
        for step in range(1, ways):
            send = lax.dynamic_index_in_dim(x, digit ^ step, 2, keepdims=False)
            pairs = [(i, i ^ (step << low)) for i in range(nseq)]
            total = total + lax.ppermute(send, "seq", pairs)
        x = total
        low += width
    x = x.reshape(-1, rows)
    for k in range(ndp.bit_length() - 1):
        x = x + lax.ppermute(x, "dp", [(i, i ^ (1 << k)) for i in range(ndp)])
    return x


def per_device(
    frames,
    frame_counts,
    clip_group,
    timesteps,
    owner_map,
    conv_weight,
    w_latent,
    hidden,
    noise,
    teacher,
    w_out,
):
    nseq = lax.axis_size("seq")
    local = frames[0]
    nframes, nrows, width, chans = local.shape
    tok_rows = nrows // 4
    tok_cols = width // 4
    per_frame = nrows * nseq // 4 * tok_cols
    counts = frame_counts[0]
    ends = jnp.cumsum(counts)
    index = jnp.arange(nframes, dtype=jnp.int32)
    clip_of = jnp.sum((index[:, None] >= ends[None, :]).astype(jnp.int32), axis=1)
    clip_hot = (clip_of[:, None] == jnp.arange(CLIPS, dtype=jnp.int32)[None, :]).astype(jnp.int32)
    starts = jnp.sum(clip_hot * (ends - counts)[None, :], axis=1)
    keep = jnp.stack([(index - lag >= starts).astype(jnp.float32) for lag in range(3)])
    rimmed = with_halo(frames, (("seq", 2),), 1)[0]
    conv = causal_conv(rimmed, conv_weight, keep)
    cells = (local.astype(jnp.float32) + jax.nn.silu(conv)).astype(jnp.bfloat16)
    tokens = lax.conv_general_dilated(
        cells,
        w_latent.reshape(4, 4, chans, LAT),
        (4, 4),
        "VALID",
        dimension_numbers=("NHWC", "HWIO", "NHWC"),
        preferred_element_type=jnp.float32,
    ).astype(jnp.bfloat16)
    latent_out = tokens.reshape(1, nframes, tok_rows, tok_cols * LAT)
    tokens = tokens.reshape(-1, LAT)
    slots = hidden.shape[1]
    capacity = slots // nseq
    assert capacity <= LAT
    owners = owner_map.reshape(-1)
    owner_hot = (owners[:, None] == jnp.arange(nseq, dtype=jnp.int32)[None, :]).astype(jnp.int32)
    rank = jnp.sum(jnp.cumsum(owner_hot, axis=0) * owner_hot, axis=1) - 1
    dest = owners * capacity + rank
    select = (dest[None, :] == jnp.arange(slots, dtype=jnp.int32)[:, None]).astype(jnp.bfloat16)
    tok_clip = jnp.repeat(clip_of, tok_rows * tok_cols).astype(jnp.float32) + 1.0
    outgoing = (
        jnp.dot(select, tokens, preferred_element_type=jnp.float32)
        .astype(jnp.bfloat16)
        .reshape(nseq, capacity, LAT)
    )
    labels = (
        jnp.dot(select, tok_clip.astype(jnp.bfloat16)[:, None], preferred_element_type=jnp.float32)
        .astype(jnp.bfloat16)
        .reshape(nseq, 1, capacity)
    )
    labels = jnp.pad(labels, ((0, 0), (0, 0), (0, LAT - capacity)))
    arrived = lax.all_to_all(
        jnp.concatenate([outgoing, labels], axis=1), "seq", split_axis=0, concat_axis=0, tiled=True
    )
    x0 = arrived[:, :capacity].reshape(slots, LAT).astype(jnp.float32)
    tag = arrived[:, capacity, :capacity].reshape(slots).astype(jnp.float32)
    kind = clip_group[0].astype(jnp.float32)
    coef = (
        (2.0 * kind - 1.0)
        * (0.1 + timesteps[0].astype(jnp.float32) / 1000.0)
        / (counts.astype(jnp.float32) * per_frame)
    )
    slot_hot = (tag[:, None] == (jnp.arange(CLIPS, dtype=jnp.float32) + 1.0)[None, :]).astype(
        jnp.float32
    )
    slot_coef = jnp.sum(slot_hot * coef[None, :], axis=1)
    slot_kind = jnp.sum(slot_hot * kind[None, :], axis=1)
    states = hidden[0].astype(jnp.float32)
    mean = jnp.mean(states, axis=1, keepdims=True)
    centred = states - mean
    var = jnp.mean(centred * centred, axis=1, keepdims=True)
    normed = (centred * lax.rsqrt(var + 1e-06)).astype(jnp.bfloat16)
    pred = jnp.dot(normed, w_out, preferred_element_type=jnp.float32)
    target = slot_kind[:, None] * teacher[0] + (1.0 - slot_kind[:, None]) * (noise[0] - x0)
    diff = pred - target
    err = jnp.sum(diff * diff, axis=1)
    partial_loss = coef * jnp.sum(slot_hot * err[:, None], axis=0)
    dpred = (2.0 * slot_coef[:, None] * diff).astype(jnp.bfloat16)
    grad_t = lax.dot_general(
        dpred, normed, (((0,), (0,)), ((), ())), preferred_element_type=jnp.float32
    )
    ndp = lax.axis_size("dp")
    share = grad_t.shape[1] // nseq
    assert ndp * CLIPS <= share
    place = lax.axis_index("dp") * CLIPS
    loss_row = lax.dynamic_update_slice(jnp.zeros((share,), jnp.float32), partial_loss, (place,))
    summed = tree_reduce(grad_t, jnp.tile(loss_row, nseq), nseq, ndp)
    grad_mine = summed[:LAT].T
    clip_loss = lax.dynamic_slice_in_dim(summed[LAT], place, CLIPS).reshape(1, CLIPS)
    return (latent_out, clip_loss, grad_mine)


def solution(mesh):
    return jax.shard_map(
        per_device,
        mesh=mesh,
        in_specs=(
            P("dp", None, "seq", None, None),
            P("dp", None),
            P("dp", None),
            P("dp", None),
            P("dp", "seq", None, None),
            P(),
            P(),
            P("dp", "seq", None),
            P("dp", "seq", None),
            P("dp", "seq", None),
            P(),
        ),
        out_specs=(P("dp", None, "seq", None), P("dp", None), P("seq", None)),
        check_vma=False,
    )
```

```python
import jax
import jax.numpy as jnp
from jax import lax
from jax.sharding import PartitionSpec as P

LAT = 64
CLIPS = 4


def with_halo(cells, sides, width):
    for axis, dim in sides:
        count = lax.axis_size(axis)
        ends = count - 1
        head = lax.slice_in_dim(cells, 0, width, axis=dim)
        tail = lax.slice_in_dim(cells, cells.shape[dim] - width, cells.shape[dim], axis=dim)
        cells = jnp.concatenate(
            [
                lax.ppermute(tail, axis, [(i, (i + 1) % count) for i in range(ends)]),
                cells,
                lax.ppermute(head, axis, [((i + 1) % count, i) for i in range(ends)]),
            ],
            axis=dim,
        )
    return cells


def causal_conv(rimmed, conv_weight, keep):
    nframes = rimmed.shape[0]
    chans = rimmed.shape[-1]
    padded = jnp.pad(rimmed, ((0, 0), (0, 0), (1, 1), (0, 0)))
    lagged = []
    for lag in range(3):
        part = jnp.pad(padded[: nframes - lag], ((lag, 0), (0, 0), (0, 0), (0, 0)))
        lagged.append(jnp.where(keep[lag][:, None, None, None] > 0, part, jnp.zeros_like(part)))
    stacked = jnp.concatenate(lagged, axis=-1)
    kernel = jnp.transpose(conv_weight, (1, 2, 0, 3, 4)).reshape(3, 3, 3 * chans, chans)
    return lax.conv_general_dilated(
        stacked,
        kernel,
        (1, 1),
        "VALID",
        dimension_numbers=("NHWC", "HWIO", "NHWC"),
        preferred_element_type=jnp.float32,
    )


def tree_reduce(grad_t, loss_line, nseq, ndp):
    rows = grad_t.shape[1] // nseq
    nbits = nseq.bit_length() - 1
    assert 1 << nbits == nseq and ndp & (ndp - 1) == 0
    groups = [1, 2] + [1] * (nbits - 3) if nbits >= 3 else [1] * nbits
    x = jnp.concatenate([grad_t, loss_line[None, :]], axis=0)
    x = x.reshape(x.shape[0], nseq, rows)
    me = lax.axis_index("seq")
    low = 0
    for width in groups:
        ways = 1 << width
        x = x.reshape(x.shape[0], x.shape[1] // ways, ways, rows)
        digit = (me >> low) & (ways - 1)
        total = lax.dynamic_index_in_dim(x, digit, 2, keepdims=False)
        for step in range(1, ways):
            send = lax.dynamic_index_in_dim(x, digit ^ step, 2, keepdims=False)
            pairs = [(i, i ^ (step << low)) for i in range(nseq)]
            total = total + lax.ppermute(send, "seq", pairs)
        x = total
        low += width
    x = x.reshape(-1, rows)
    for k in range(ndp.bit_length() - 1):
        x = x + lax.ppermute(x, "dp", [(i, i ^ (1 << k)) for i in range(ndp)])
    return x


def per_device(
    frames,
    frame_counts,
    clip_group,
    timesteps,
    owner_map,
    conv_weight,
    w_latent,
    hidden,
    noise,
    teacher,
    w_out,
):
    nseq = lax.axis_size("seq")
    local = frames[0]
    nframes, nrows, width, chans = local.shape
    tok_rows = nrows // 4
    tok_cols = width // 4
    per_frame = nrows * nseq // 4 * tok_cols
    counts = frame_counts[0]
    ends = jnp.cumsum(counts)
    index = jnp.arange(nframes, dtype=jnp.int32)
    clip_of = jnp.sum((index[:, None] >= ends[None, :]).astype(jnp.int32), axis=1)
    clip_hot = (clip_of[:, None] == jnp.arange(CLIPS, dtype=jnp.int32)[None, :]).astype(jnp.int32)
    starts = jnp.sum(clip_hot * (ends - counts)[None, :], axis=1)
    keep = jnp.stack([(index - lag >= starts).astype(jnp.float32) for lag in range(3)])
    rimmed = with_halo(frames, (("seq", 2),), 1)[0]
    conv = causal_conv(rimmed, conv_weight, keep)
    cells = (local.astype(jnp.float32) + jax.nn.silu(conv)).astype(jnp.bfloat16)
    tokens = lax.conv_general_dilated(
        cells,
        w_latent.reshape(4, 4, chans, LAT),
        (4, 4),
        "VALID",
        dimension_numbers=("NHWC", "HWIO", "NHWC"),
        preferred_element_type=jnp.float32,
    ).astype(jnp.bfloat16)
    latent_out = tokens.reshape(1, nframes, tok_rows, tok_cols * LAT)
    tokens = tokens.reshape(-1, LAT)
    slots = hidden.shape[1]
    capacity = slots // nseq
    assert capacity <= LAT
    owners = owner_map.reshape(-1)
    owner_hot = (owners[:, None] == jnp.arange(nseq, dtype=jnp.int32)[None, :]).astype(jnp.int32)
    rank = jnp.sum(jnp.cumsum(owner_hot, axis=0) * owner_hot, axis=1) - 1
    dest = owners * capacity + rank
    select = (dest[None, :] == jnp.arange(slots, dtype=jnp.int32)[:, None]).astype(jnp.bfloat16)
    tok_clip = jnp.repeat(clip_of, tok_rows * tok_cols).astype(jnp.float32) + 1.0
    outgoing = (
        jnp.dot(select, tokens, preferred_element_type=jnp.float32)
        .astype(jnp.bfloat16)
        .reshape(nseq, capacity, LAT)
    )
    labels = (
        jnp.dot(select, tok_clip.astype(jnp.bfloat16)[:, None], preferred_element_type=jnp.float32)
        .astype(jnp.bfloat16)
        .reshape(nseq, 1, capacity)
    )
    labels = jnp.pad(labels, ((0, 0), (0, 0), (0, LAT - capacity)))
    arrived = lax.all_to_all(
        jnp.concatenate([outgoing, labels], axis=1), "seq", split_axis=0, concat_axis=0, tiled=True
    )
    x0 = arrived[:, :capacity].reshape(slots, LAT).astype(jnp.float32)
    tag = arrived[:, capacity, :capacity].reshape(slots).astype(jnp.float32)
    kind = clip_group[0].astype(jnp.float32)
    coef = (
        (2.0 * kind - 1.0)
        * (0.1 + timesteps[0].astype(jnp.float32) / 1000.0)
        / (counts.astype(jnp.float32) * per_frame)
    )
    slot_hot = (tag[:, None] == (jnp.arange(CLIPS, dtype=jnp.float32) + 1.0)[None, :]).astype(
        jnp.float32
    )
    slot_coef = jnp.sum(slot_hot * coef[None, :], axis=1)
    slot_kind = jnp.sum(slot_hot * kind[None, :], axis=1)
    states = hidden[0].astype(jnp.float32)
    mean = jnp.mean(states, axis=1, keepdims=True)
    centred = states - mean
    var = jnp.mean(centred * centred, axis=1, keepdims=True)
    normed = (centred * lax.rsqrt(var + 1e-06)).astype(jnp.bfloat16)
    pred = jnp.dot(normed, w_out, preferred_element_type=jnp.float32)
    target = slot_kind[:, None] * teacher[0] + (1.0 - slot_kind[:, None]) * (noise[0] - x0)
    diff = pred - target
    err = jnp.sum(diff * diff, axis=1)
    partial_loss = coef * jnp.sum(slot_hot * err[:, None], axis=0)
    dpred = (2.0 * slot_coef[:, None] * diff).astype(jnp.bfloat16)
    grad_t = lax.dot_general(
        dpred, normed, (((0,), (0,)), ((), ())), preferred_element_type=jnp.float32
    )
    ndp = lax.axis_size("dp")
    share = grad_t.shape[1] // nseq
    assert ndp * CLIPS <= share
    place = lax.axis_index("dp") * CLIPS
    loss_row = lax.dynamic_update_slice(jnp.zeros((share,), jnp.float32), partial_loss, (place,))
    summed = tree_reduce(grad_t, jnp.tile(loss_row, nseq), nseq, ndp)
    grad_mine = summed[:LAT].T
    clip_loss = lax.dynamic_slice_in_dim(summed[LAT], place, CLIPS).reshape(1, CLIPS)
    return (latent_out, clip_loss, grad_mine)


def solution(mesh):
    return jax.shard_map(
        per_device,
        mesh=mesh,
        in_specs=(
            P("dp", None, "seq", None, None),
            P("dp", None),
            P("dp", None),
            P("dp", None),
            P("dp", "seq", None, None),
            P(),
            P(),
            P("dp", "seq", None),
            P("dp", "seq", None),
            P("dp", "seq", None),
            P(),
        ),
        out_specs=(P("dp", None, "seq", None), P("dp", None), P("seq", None)),
        check_vma=False,
    )
```

```python
import jax
import jax.numpy as jnp
from jax import lax
from jax.sharding import PartitionSpec as P

LAT = 64
CLIPS = 4


def with_halo(cells, sides, width):
    for axis, dim in sides:
        count = lax.axis_size(axis)
        ends = count - 1
        head = lax.slice_in_dim(cells, 0, width, axis=dim)
        tail = lax.slice_in_dim(cells, cells.shape[dim] - width, cells.shape[dim], axis=dim)
        cells = jnp.concatenate(
            [
                lax.ppermute(tail, axis, [(i, (i + 1) % count) for i in range(ends)]),
                cells,
                lax.ppermute(head, axis, [((i + 1) % count, i) for i in range(ends)]),
            ],
            axis=dim,
        )
    return cells


def causal_conv(rimmed, conv_weight, keep):
    nframes = rimmed.shape[0]
    chans = rimmed.shape[-1]
    padded = jnp.pad(rimmed, ((0, 0), (0, 0), (1, 1), (0, 0)))
    kernel = jnp.transpose(conv_weight, (1, 2, 3, 0, 4)).reshape(3, 3, chans, 3 * chans)
    each = lax.conv_general_dilated(
        padded,
        kernel,
        (1, 1),
        "VALID",
        dimension_numbers=("NHWC", "HWIO", "NHWC"),
        preferred_element_type=jnp.float32,
    )
    total = each[..., :chans]
    for lag in (1, 2):
        part = each[: nframes - lag, ..., lag * chans : (lag + 1) * chans]
        part = jnp.pad(part, ((lag, 0), (0, 0), (0, 0), (0, 0)))
        total = total + part * keep[lag][:, None, None, None]
    return total


def tree_reduce(blocks, nseq, ndp):
    nbits = nseq.bit_length() - 1
    assert 1 << nbits == nseq and ndp & (ndp - 1) == 0
    groups = [1, 2] + [1] * (nbits - 3) if nbits >= 3 else [1] * nbits
    x = blocks
    tail = x.shape[1:]
    me = lax.axis_index("seq")
    low = 0
    for width in groups:
        ways = 1 << width
        x = x.reshape((x.shape[0] // ways, ways) + tail)
        digit = (me >> low) & (ways - 1)
        total = lax.dynamic_index_in_dim(x, digit, 1, keepdims=False)
        for step in range(1, ways):
            send = lax.dynamic_index_in_dim(x, digit ^ step, 1, keepdims=False)
            pairs = [(i, i ^ (step << low)) for i in range(nseq)]
            total = total + lax.ppermute(send, "seq", pairs)
        x = total
        low += width
    x = x.reshape(tail)
    for k in range(ndp.bit_length() - 1):
        x = x + lax.ppermute(x, "dp", [(i, i ^ (1 << k)) for i in range(ndp)])
    return x


def per_device(
    frames,
    frame_counts,
    clip_group,
    timesteps,
    owner_map,
    conv_weight,
    w_latent,
    hidden,
    noise,
    teacher,
    w_out,
):
    nseq = lax.axis_size("seq")
    local = frames[0]
    nframes, nrows, width, chans = local.shape
    tok_rows = nrows // 4
    tok_cols = width // 4
    per_frame = nrows * nseq // 4 * tok_cols
    counts = frame_counts[0]
    ends = jnp.cumsum(counts)
    index = jnp.arange(nframes, dtype=jnp.int32)
    clip_of = jnp.sum((index[:, None] >= ends[None, :]).astype(jnp.int32), axis=1)
    clip_hot = (clip_of[:, None] == jnp.arange(CLIPS, dtype=jnp.int32)[None, :]).astype(jnp.int32)
    starts = jnp.sum(clip_hot * (ends - counts)[None, :], axis=1)
    keep = jnp.stack([(index - lag >= starts).astype(jnp.float32) for lag in range(3)])
    rimmed = with_halo(frames, (("seq", 2),), 1)[0]
    conv = causal_conv(rimmed, conv_weight, keep)
    cells = (local.astype(jnp.float32) + jax.nn.silu(conv)).astype(jnp.bfloat16)
    tokens = lax.conv_general_dilated(
        cells,
        w_latent.reshape(4, 4, chans, LAT),
        (4, 4),
        "VALID",
        dimension_numbers=("NHWC", "HWIO", "NHWC"),
        preferred_element_type=jnp.float32,
    ).astype(jnp.bfloat16)
    latent_out = tokens.reshape(1, nframes, tok_rows, tok_cols * LAT)
    tokens = tokens.reshape(-1, LAT)
    slots = hidden.shape[1]
    capacity = slots // nseq
    assert capacity <= LAT
    owners = owner_map.reshape(-1)
    owner_hot = (owners[:, None] == jnp.arange(nseq, dtype=jnp.int32)[None, :]).astype(jnp.int32)
    rank = jnp.sum(jnp.cumsum(owner_hot, axis=0) * owner_hot, axis=1) - 1
    dest = owners * capacity + rank
    select = (dest[None, :] == jnp.arange(slots, dtype=jnp.int32)[:, None]).astype(jnp.bfloat16)
    tok_clip = jnp.repeat(clip_of, tok_rows * tok_cols).astype(jnp.float32) + 1.0
    outgoing = (
        jnp.dot(select, tokens, preferred_element_type=jnp.float32)
        .astype(jnp.bfloat16)
        .reshape(nseq, capacity, LAT)
    )
    labels = (
        jnp.dot(select, tok_clip.astype(jnp.bfloat16)[:, None], preferred_element_type=jnp.float32)
        .astype(jnp.bfloat16)
        .reshape(nseq, 1, capacity)
    )
    labels = jnp.pad(labels, ((0, 0), (0, 0), (0, LAT - capacity)))
    arrived = lax.all_to_all(
        jnp.concatenate([outgoing, labels], axis=1), "seq", split_axis=0, concat_axis=0, tiled=True
    )
    x0 = arrived[:, :capacity].reshape(slots, LAT).astype(jnp.float32)
    tag = arrived[:, capacity, :capacity].reshape(slots).astype(jnp.float32)
    kind = clip_group[0].astype(jnp.float32)
    coef = (
        (2.0 * kind - 1.0)
        * (0.1 + timesteps[0].astype(jnp.float32) / 1000.0)
        / (counts.astype(jnp.float32) * per_frame)
    )
    slot_hot = (tag[:, None] == (jnp.arange(CLIPS, dtype=jnp.float32) + 1.0)[None, :]).astype(
        jnp.float32
    )
    slot_coef = jnp.sum(slot_hot * coef[None, :], axis=1)
    slot_kind = jnp.sum(slot_hot * kind[None, :], axis=1)
    states = hidden[0].astype(jnp.float32)
    mean = jnp.mean(states, axis=1, keepdims=True)
    centred = states - mean
    var = jnp.mean(centred * centred, axis=1, keepdims=True)
    normed = (centred * lax.rsqrt(var + 1e-06)).astype(jnp.bfloat16)
    pred = jnp.dot(normed, w_out, preferred_element_type=jnp.float32)
    target = slot_kind[:, None] * teacher[0] + (1.0 - slot_kind[:, None]) * (noise[0] - x0)
    diff = pred - target
    err = jnp.sum(diff * diff, axis=1)
    partial_loss = coef * jnp.sum(slot_hot * err[:, None], axis=0)
    dpred = (2.0 * slot_coef[:, None] * diff).astype(jnp.bfloat16)
    grad_t = lax.dot_general(
        dpred, normed, (((0,), (0,)), ((), ())), preferred_element_type=jnp.float32
    )
    ndp = lax.axis_size("dp")
    share = grad_t.shape[1] // nseq
    lanes = 128
    dense = LAT * share // lanes
    assert ndp * CLIPS <= lanes and dense * lanes == LAT * share
    place = lax.axis_index("dp") * CLIPS
    blocks = grad_t.reshape(LAT, nseq, share).transpose(1, 0, 2).reshape(nseq, dense, lanes)
    loss_row = lax.dynamic_update_slice(jnp.zeros((lanes,), jnp.float32), partial_loss, (place,))
    loss_rows = jnp.broadcast_to(loss_row[None, None, :], (nseq, 1, lanes))
    summed = tree_reduce(jnp.concatenate([blocks, loss_rows], axis=1), nseq, ndp)
    grad_mine = summed[:dense].reshape(LAT, share).T
    clip_loss = lax.dynamic_slice_in_dim(summed[dense], place, CLIPS).reshape(1, CLIPS)
    return (latent_out, clip_loss, grad_mine)


def solution(mesh):
    return jax.shard_map(
        per_device,
        mesh=mesh,
        in_specs=(
            P("dp", None, "seq", None, None),
            P("dp", None),
            P("dp", None),
            P("dp", None),
            P("dp", "seq", None, None),
            P(),
            P(),
            P("dp", "seq", None),
            P("dp", "seq", None),
            P("dp", "seq", None),
            P(),
        ),
        out_specs=(P("dp", None, "seq", None), P("dp", None), P("seq", None)),
        check_vma=False,
    )
```

```python
import jax
import jax.numpy as jnp
from jax import lax
from jax.sharding import PartitionSpec as P

LAT = 64
CLIPS = 4


def with_halo(cells, sides, width):
    for axis, dim in sides:
        count = lax.axis_size(axis)
        ends = count - 1
        head = lax.slice_in_dim(cells, 0, width, axis=dim)
        tail = lax.slice_in_dim(cells, cells.shape[dim] - width, cells.shape[dim], axis=dim)
        cells = jnp.concatenate(
            [
                lax.ppermute(tail, axis, [(i, (i + 1) % count) for i in range(ends)]),
                cells,
                lax.ppermute(head, axis, [((i + 1) % count, i) for i in range(ends)]),
            ],
            axis=dim,
        )
    return cells


def causal_conv(rimmed, conv_weight, keep):
    nframes = rimmed.shape[0]
    chans = rimmed.shape[-1]
    padded = jnp.pad(rimmed, ((0, 0), (0, 0), (1, 1), (0, 0)))
    kernel = jnp.transpose(conv_weight, (1, 2, 3, 0, 4)).reshape(3, 3, chans, 3 * chans)
    each = lax.conv_general_dilated(
        padded,
        kernel,
        (1, 1),
        "VALID",
        dimension_numbers=("NHWC", "HWIO", "NHWC"),
        preferred_element_type=jnp.float32,
    )
    total = each[..., :chans]
    for lag in (1, 2):
        part = each[: nframes - lag, ..., lag * chans : (lag + 1) * chans]
        part = jnp.pad(part, ((lag, 0), (0, 0), (0, 0), (0, 0)))
        total = total + part * keep[lag][:, None, None, None]
    return total


def tree_reduce(grad_t, loss_row, nseq, ndp):
    nbits = nseq.bit_length() - 1
    assert nbits >= 1 and 1 << nbits == nseq and ndp & (ndp - 1) == 0
    groups = [2] + [1] * (nbits - 3) if nbits >= 3 else [1] * (nbits - 1)
    lat = grad_t.shape[0]
    share = grad_t.shape[1] // nseq
    lanes = loss_row.shape[0]
    dense = lat * share // lanes
    me = lax.axis_index("seq")
    halves = grad_t.reshape(lat, nseq // 2, 2, share)
    loss_rows = jnp.broadcast_to(loss_row[None, None, :], (nseq // 2, 1, lanes))

    def half(bit):
        part = lax.dynamic_index_in_dim(halves, bit, 2, keepdims=False)
        part = part.transpose(1, 0, 2).reshape(nseq // 2, dense, lanes)
        return jnp.concatenate([part, loss_rows], axis=1)

    bit = me & 1
    x = half(bit) + lax.ppermute(half(1 - bit), "seq", [(i, i ^ 1) for i in range(nseq)])
    tail = x.shape[1:]
    low = 1
    for width in groups:
        ways = 1 << width
        x = x.reshape((x.shape[0] // ways, ways) + tail)
        digit = (me >> low) & (ways - 1)
        total = lax.dynamic_index_in_dim(x, digit, 1, keepdims=False)
        for step in range(1, ways):
            send = lax.dynamic_index_in_dim(x, digit ^ step, 1, keepdims=False)
            pairs = [(i, i ^ (step << low)) for i in range(nseq)]
            total = total + lax.ppermute(send, "seq", pairs)
        x = total
        low += width
    x = x.reshape(tail)
    for k in range(ndp.bit_length() - 1):
        x = x + lax.ppermute(x, "dp", [(i, i ^ (1 << k)) for i in range(ndp)])
    return x


def per_device(
    frames,
    frame_counts,
    clip_group,
    timesteps,
    owner_map,
    conv_weight,
    w_latent,
    hidden,
    noise,
    teacher,
    w_out,
):
    nseq = lax.axis_size("seq")
    local = frames[0]
    nframes, nrows, width, chans = local.shape
    tok_rows = nrows // 4
    tok_cols = width // 4
    per_frame = nrows * nseq // 4 * tok_cols
    counts = frame_counts[0]
    ends = jnp.cumsum(counts)
    index = jnp.arange(nframes, dtype=jnp.int32)
    clip_of = jnp.sum((index[:, None] >= ends[None, :]).astype(jnp.int32), axis=1)
    clip_hot = (clip_of[:, None] == jnp.arange(CLIPS, dtype=jnp.int32)[None, :]).astype(jnp.int32)
    starts = jnp.sum(clip_hot * (ends - counts)[None, :], axis=1)
    keep = jnp.stack([(index - lag >= starts).astype(jnp.float32) for lag in range(3)])
    rimmed = with_halo(frames, (("seq", 2),), 1)[0]
    conv = causal_conv(rimmed, conv_weight, keep)
    cells = (local.astype(jnp.float32) + jax.nn.silu(conv)).astype(jnp.bfloat16)
    tokens = lax.conv_general_dilated(
        cells,
        w_latent.reshape(4, 4, chans, LAT),
        (4, 4),
        "VALID",
        dimension_numbers=("NHWC", "HWIO", "NHWC"),
        preferred_element_type=jnp.float32,
    ).astype(jnp.bfloat16)
    latent_out = tokens.reshape(1, nframes, tok_rows, tok_cols * LAT)
    tokens = tokens.reshape(-1, LAT)
    slots = hidden.shape[1]
    capacity = slots // nseq
    assert capacity <= LAT
    owners = owner_map.reshape(-1)
    owner_hot = (owners[:, None] == jnp.arange(nseq, dtype=jnp.int32)[None, :]).astype(jnp.int32)
    rank = jnp.sum(jnp.cumsum(owner_hot, axis=0) * owner_hot, axis=1) - 1
    dest = owners * capacity + rank
    select = (dest[None, :] == jnp.arange(slots, dtype=jnp.int32)[:, None]).astype(jnp.bfloat16)
    tok_clip = jnp.repeat(clip_of, tok_rows * tok_cols).astype(jnp.float32) + 1.0
    outgoing = (
        jnp.dot(select, tokens, preferred_element_type=jnp.float32)
        .astype(jnp.bfloat16)
        .reshape(nseq, capacity, LAT)
    )
    labels = (
        jnp.dot(select, tok_clip.astype(jnp.bfloat16)[:, None], preferred_element_type=jnp.float32)
        .astype(jnp.bfloat16)
        .reshape(nseq, 1, capacity)
    )
    labels = jnp.pad(labels, ((0, 0), (0, 0), (0, LAT - capacity)))
    arrived = lax.all_to_all(
        jnp.concatenate([outgoing, labels], axis=1), "seq", split_axis=0, concat_axis=0, tiled=True
    )
    x0 = arrived[:, :capacity].reshape(slots, LAT).astype(jnp.float32)
    tag = arrived[:, capacity, :capacity].reshape(slots).astype(jnp.float32)
    kind = clip_group[0].astype(jnp.float32)
    coef = (
        (2.0 * kind - 1.0)
        * (0.1 + timesteps[0].astype(jnp.float32) / 1000.0)
        / (counts.astype(jnp.float32) * per_frame)
    )
    slot_hot = (tag[:, None] == (jnp.arange(CLIPS, dtype=jnp.float32) + 1.0)[None, :]).astype(
        jnp.float32
    )
    slot_coef = jnp.sum(slot_hot * coef[None, :], axis=1)
    slot_kind = jnp.sum(slot_hot * kind[None, :], axis=1)
    states = hidden[0].astype(jnp.float32)
    mean = jnp.mean(states, axis=1, keepdims=True)
    centred = states - mean
    var = jnp.mean(centred * centred, axis=1, keepdims=True)
    normed = (centred * lax.rsqrt(var + 1e-06)).astype(jnp.bfloat16)
    pred = jnp.dot(normed, w_out, preferred_element_type=jnp.float32)
    target = slot_kind[:, None] * teacher[0] + (1.0 - slot_kind[:, None]) * (noise[0] - x0)
    diff = pred - target
    err = jnp.sum(diff * diff, axis=1)
    partial_loss = coef * jnp.sum(slot_hot * err[:, None], axis=0)
    dpred = (2.0 * slot_coef[:, None] * diff).astype(jnp.bfloat16)
    grad_t = lax.dot_general(
        dpred, normed, (((0,), (0,)), ((), ())), preferred_element_type=jnp.float32
    )
    ndp = lax.axis_size("dp")
    share = grad_t.shape[1] // nseq
    lanes = 128
    dense = LAT * share // lanes
    assert ndp * CLIPS <= lanes and dense * lanes == LAT * share
    place = lax.axis_index("dp") * CLIPS
    loss_row = lax.dynamic_update_slice(jnp.zeros((lanes,), jnp.float32), partial_loss, (place,))
    summed = tree_reduce(grad_t, loss_row, nseq, ndp)
    grad_mine = summed[:dense].reshape(LAT, share).T
    clip_loss = lax.dynamic_slice_in_dim(summed[dense], place, CLIPS).reshape(1, CLIPS)
    return (latent_out, clip_loss, grad_mine)


def solution(mesh):
    return jax.shard_map(
        per_device,
        mesh=mesh,
        in_specs=(
            P("dp", None, "seq", None, None),
            P("dp", None),
            P("dp", None),
            P("dp", None),
            P("dp", "seq", None, None),
            P(),
            P(),
            P("dp", "seq", None),
            P("dp", "seq", None),
            P("dp", "seq", None),
            P(),
        ),
        out_specs=(P("dp", None, "seq", None), P("dp", None), P("seq", None)),
        check_vma=False,
    )
```

```python
import jax
import jax.numpy as jnp
from jax import lax
from jax.sharding import PartitionSpec as P

LAT = 64
CLIPS = 4


def with_halo(cells, sides, width):
    for axis, dim in sides:
        count = lax.axis_size(axis)
        ends = count - 1
        head = lax.slice_in_dim(cells, 0, width, axis=dim)
        tail = lax.slice_in_dim(cells, cells.shape[dim] - width, cells.shape[dim], axis=dim)
        cells = jnp.concatenate(
            [
                lax.ppermute(tail, axis, [(i, (i + 1) % count) for i in range(ends)]),
                cells,
                lax.ppermute(head, axis, [((i + 1) % count, i) for i in range(ends)]),
            ],
            axis=dim,
        )
    return cells


def causal_conv(rimmed, conv_weight, keep):
    nframes = rimmed.shape[0]
    chans = rimmed.shape[-1]
    padded = jnp.pad(rimmed, ((0, 0), (0, 0), (1, 1), (0, 0)))
    kernel = jnp.transpose(conv_weight, (1, 2, 3, 0, 4)).reshape(3, 3, chans, 3 * chans)
    each = lax.conv_general_dilated(
        padded,
        kernel,
        (1, 1),
        "VALID",
        dimension_numbers=("NHWC", "HWIO", "NHWC"),
        preferred_element_type=jnp.float32,
    )
    total = each[..., :chans]
    for lag in (1, 2):
        part = each[: nframes - lag, ..., lag * chans : (lag + 1) * chans]
        part = jnp.pad(part, ((lag, 0), (0, 0), (0, 0), (0, 0)))
        total = total + part * keep[lag][:, None, None, None]
    return total


def tree_reduce(grad_t, loss_row, nseq, ndp):
    nbits = nseq.bit_length() - 1
    assert nbits >= 1 and 1 << nbits == nseq and ndp & (ndp - 1) == 0
    groups = [2] + [1] * (nbits - 3) if nbits >= 3 else [1] * (nbits - 1)
    lat = grad_t.shape[0]
    share = grad_t.shape[1] // nseq
    lanes = loss_row.shape[0]
    dense = lat * share // lanes
    me = lax.axis_index("seq")
    halves = grad_t.reshape(lat, nseq // 2, 2, share)
    loss_rows = jnp.broadcast_to(loss_row[None, None, :], (nseq // 2, 1, lanes))

    def half(bit):
        part = lax.dynamic_index_in_dim(halves, bit, 2, keepdims=False)
        part = part.transpose(1, 0, 2).reshape(nseq // 2, dense, lanes)
        return jnp.concatenate([part, loss_rows], axis=1)

    bit = me & 1
    x = half(bit) + lax.ppermute(half(1 - bit), "seq", [(i, i ^ 1) for i in range(nseq)])
    tail = x.shape[1:]
    low = 1
    for width in groups:
        ways = 1 << width
        x = x.reshape((x.shape[0] // ways, ways) + tail)
        digit = (me >> low) & (ways - 1)
        total = lax.dynamic_index_in_dim(x, digit, 1, keepdims=False)
        for step in range(1, ways):
            send = lax.dynamic_index_in_dim(x, digit ^ step, 1, keepdims=False)
            pairs = [(i, i ^ (step << low)) for i in range(nseq)]
            total = total + lax.ppermute(send, "seq", pairs)
        x = total
        low += width
    x = x.reshape(tail)
    for k in range(ndp.bit_length() - 1):
        x = x + lax.ppermute(x, "dp", [(i, i ^ (1 << k)) for i in range(ndp)])
    return x


def per_device(
    frames,
    frame_counts,
    clip_group,
    timesteps,
    owner_map,
    conv_weight,
    w_latent,
    hidden,
    noise,
    teacher,
    w_out,
):
    nseq = lax.axis_size("seq")
    local = frames[0]
    nframes, nrows, width, chans = local.shape
    tok_rows = nrows // 4
    tok_cols = width // 4
    per_frame = nrows * nseq // 4 * tok_cols
    counts = frame_counts[0]
    ends = jnp.cumsum(counts)
    index = jnp.arange(nframes, dtype=jnp.int32)
    clip_of = jnp.sum((index[:, None] >= ends[None, :]).astype(jnp.int32), axis=1)
    clip_hot = (clip_of[:, None] == jnp.arange(CLIPS, dtype=jnp.int32)[None, :]).astype(jnp.int32)
    starts = jnp.sum(clip_hot * (ends - counts)[None, :], axis=1)
    keep = jnp.stack([(index - lag >= starts).astype(jnp.float32) for lag in range(3)])
    rimmed = with_halo(frames, (("seq", 2),), 1)[0]
    conv = causal_conv(rimmed, conv_weight, keep)
    cells = (local.astype(jnp.float32) + jax.nn.silu(conv)).astype(jnp.bfloat16)
    tokens = lax.conv_general_dilated(
        cells,
        w_latent.reshape(4, 4, chans, LAT),
        (4, 4),
        "VALID",
        dimension_numbers=("NHWC", "HWIO", "NHWC"),
        preferred_element_type=jnp.float32,
    ).astype(jnp.bfloat16)
    latent_out = tokens.reshape(1, nframes, tok_rows, tok_cols * LAT)
    tokens = tokens.reshape(-1, LAT)
    slots = hidden.shape[1]
    capacity = slots // nseq
    assert capacity <= LAT
    owners = owner_map.reshape(-1)
    owner_hot = (owners[:, None] == jnp.arange(nseq, dtype=jnp.int32)[None, :]).astype(jnp.int32)
    rank = jnp.sum(jnp.cumsum(owner_hot, axis=0) * owner_hot, axis=1) - 1
    dest = owners * capacity + rank
    select = (dest[None, :] == jnp.arange(slots, dtype=jnp.int32)[:, None]).astype(jnp.bfloat16)
    tok_clip = jnp.repeat(clip_of, tok_rows * tok_cols).astype(jnp.float32) + 1.0
    outgoing = (
        jnp.dot(select, tokens, preferred_element_type=jnp.float32)
        .astype(jnp.bfloat16)
        .reshape(nseq, capacity, LAT)
    )
    labels = (
        jnp.dot(select, tok_clip.astype(jnp.bfloat16)[:, None], preferred_element_type=jnp.float32)
        .astype(jnp.bfloat16)
        .reshape(nseq, 1, capacity)
    )
    labels = jnp.pad(labels, ((0, 0), (0, 0), (0, LAT - capacity)))
    arrived = lax.all_to_all(
        jnp.concatenate([outgoing, labels], axis=1), "seq", split_axis=0, concat_axis=0, tiled=True
    )
    x0 = arrived[:, :capacity].reshape(slots, LAT).astype(jnp.float32)
    tag = arrived[:, capacity, :capacity].reshape(slots).astype(jnp.float32)
    kind = clip_group[0].astype(jnp.float32)
    coef = (
        (2.0 * kind - 1.0)
        * (0.1 + timesteps[0].astype(jnp.float32) / 1000.0)
        / (counts.astype(jnp.float32) * per_frame)
    )
    slot_hot = (tag[:, None] == (jnp.arange(CLIPS, dtype=jnp.float32) + 1.0)[None, :]).astype(
        jnp.float32
    )
    slot_coef = jnp.sum(slot_hot * coef[None, :], axis=1)
    slot_kind = jnp.sum(slot_hot * kind[None, :], axis=1)
    states = hidden[0].astype(jnp.float32)
    mean = jnp.mean(states, axis=1, keepdims=True)
    centred = states - mean
    var = jnp.mean(centred * centred, axis=1, keepdims=True)
    normed = (centred * lax.rsqrt(var + 1e-06)).astype(jnp.bfloat16)
    pred = jnp.dot(normed, w_out, preferred_element_type=jnp.float32)
    target = slot_kind[:, None] * teacher[0] + (1.0 - slot_kind[:, None]) * (noise[0] - x0)
    diff = pred - target
    err = jnp.sum(diff * diff, axis=1)
    partial_loss = coef * jnp.sum(slot_hot * err[:, None], axis=0)
    dpred = (2.0 * slot_coef[:, None] * diff).astype(jnp.bfloat16)
    states_t = hidden[0].T.astype(jnp.float32)
    normed_t = ((states_t - mean.T) * lax.rsqrt(var.T + 1e-06)).astype(jnp.bfloat16)
    grad_t = lax.dot_general(
        dpred, normed_t, (((0,), (1,)), ((), ())), preferred_element_type=jnp.float32
    )
    ndp = lax.axis_size("dp")
    share = grad_t.shape[1] // nseq
    lanes = 128
    dense = LAT * share // lanes
    assert ndp * CLIPS <= lanes and dense * lanes == LAT * share
    place = lax.axis_index("dp") * CLIPS
    loss_row = lax.dynamic_update_slice(jnp.zeros((lanes,), jnp.float32), partial_loss, (place,))
    summed = tree_reduce(grad_t, loss_row, nseq, ndp)
    grad_mine = summed[:dense].reshape(LAT, share).T
    clip_loss = lax.dynamic_slice_in_dim(summed[dense], place, CLIPS).reshape(1, CLIPS)
    return (latent_out, clip_loss, grad_mine)


def solution(mesh):
    return jax.shard_map(
        per_device,
        mesh=mesh,
        in_specs=(
            P("dp", None, "seq", None, None),
            P("dp", None),
            P("dp", None),
            P("dp", None),
            P("dp", "seq", None, None),
            P(),
            P(),
            P("dp", "seq", None),
            P("dp", "seq", None),
            P("dp", "seq", None),
            P(),
        ),
        out_specs=(P("dp", None, "seq", None), P("dp", None), P("seq", None)),
        check_vma=False,
    )
```

```python
import jax
import jax.numpy as jnp
from jax import lax
from jax.sharding import PartitionSpec as P

LAT = 64
CLIPS = 4


def with_halo(cells, sides, width):
    for axis, dim in sides:
        count = lax.axis_size(axis)
        ends = count - 1
        head = lax.slice_in_dim(cells, 0, width, axis=dim)
        tail = lax.slice_in_dim(cells, cells.shape[dim] - width, cells.shape[dim], axis=dim)
        cells = jnp.concatenate(
            [
                lax.ppermute(tail, axis, [(i, (i + 1) % count) for i in range(ends)]),
                cells,
                lax.ppermute(head, axis, [((i + 1) % count, i) for i in range(ends)]),
            ],
            axis=dim,
        )
    return cells


def causal_conv(rimmed, conv_weight, keep):
    nframes = rimmed.shape[0]
    chans = rimmed.shape[-1]
    padded = jnp.pad(rimmed, ((0, 0), (0, 0), (1, 1), (0, 0)))
    kernel = jnp.transpose(conv_weight, (1, 2, 3, 0, 4)).reshape(3, 3, chans, 3 * chans)
    each = lax.conv_general_dilated(
        padded,
        kernel,
        (1, 1),
        "VALID",
        dimension_numbers=("NHWC", "HWIO", "NHWC"),
        preferred_element_type=jnp.float32,
    )
    total = each[..., :chans]
    for lag in (1, 2):
        part = each[: nframes - lag, ..., lag * chans : (lag + 1) * chans]
        part = jnp.pad(part, ((lag, 0), (0, 0), (0, 0), (0, 0)))
        total = total + part * keep[lag][:, None, None, None]
    return total


def tree_reduce(grad_t, loss_row, nseq, ndp):
    nbits = nseq.bit_length() - 1
    assert nbits >= 1 and 1 << nbits == nseq and ndp & (ndp - 1) == 0
    groups = [2] + [1] * (nbits - 3) if nbits >= 3 else [1] * (nbits - 1)
    lat = grad_t.shape[0]
    share = grad_t.shape[1] // nseq
    lanes = loss_row.shape[0]
    dense = lat * share // lanes
    me = lax.axis_index("seq")
    halves = grad_t.reshape(lat, nseq // 2, 2, share)
    loss_rows = jnp.broadcast_to(loss_row[None, None, :], (nseq // 2, 1, lanes))

    def half(bit):
        part = lax.dynamic_index_in_dim(halves, bit, 2, keepdims=False)
        part = part.transpose(1, 0, 2).reshape(nseq // 2, dense, lanes)
        return jnp.concatenate([part, loss_rows], axis=1)

    bit = me & 1
    x = half(bit) + lax.ppermute(half(1 - bit), "seq", [(i, i ^ 1) for i in range(nseq)])
    tail = x.shape[1:]
    low = 1
    for width in groups:
        ways = 1 << width
        x = x.reshape((x.shape[0] // ways, ways) + tail)
        digit = (me >> low) & (ways - 1)
        total = lax.dynamic_index_in_dim(x, digit, 1, keepdims=False)
        for step in range(1, ways):
            send = lax.dynamic_index_in_dim(x, digit ^ step, 1, keepdims=False)
            pairs = [(i, i ^ (step << low)) for i in range(nseq)]
            total = total + lax.ppermute(send, "seq", pairs)
        x = total
        low += width
    x = x.reshape(tail)
    for k in range(ndp.bit_length() - 1):
        x = x + lax.ppermute(x, "dp", [(i, i ^ (1 << k)) for i in range(ndp)])
    return x


def per_device(
    frames,
    frame_counts,
    clip_group,
    timesteps,
    owner_map,
    conv_weight,
    w_latent,
    hidden,
    noise,
    teacher,
    w_out,
):
    nseq = lax.axis_size("seq")
    nframes, nrows, width, chans = frames.shape[1:]
    tok_rows = nrows // 4
    tok_cols = width // 4
    per_frame = nrows * nseq // 4 * tok_cols
    counts = frame_counts[0]
    ends = jnp.cumsum(counts)
    index = jnp.arange(nframes, dtype=jnp.int32)
    clip_of = jnp.sum((index[:, None] >= ends[None, :]).astype(jnp.int32), axis=1)
    clip_hot = (clip_of[:, None] == jnp.arange(CLIPS, dtype=jnp.int32)[None, :]).astype(jnp.int32)
    starts = jnp.sum(clip_hot * (ends - counts)[None, :], axis=1)
    keep = jnp.stack([(index - lag >= starts).astype(jnp.float32) for lag in range(3)])
    slots = hidden.shape[1]
    capacity = slots // nseq
    assert capacity <= LAT
    owners = owner_map.reshape(-1)
    owner_hot = (owners[:, None] == jnp.arange(nseq, dtype=jnp.int32)[None, :]).astype(jnp.int32)
    rank = jnp.sum(jnp.cumsum(owner_hot, axis=0) * owner_hot, axis=1) - 1
    dest = owners * capacity + rank
    select = (dest[None, :] == jnp.arange(slots, dtype=jnp.int32)[:, None]).astype(jnp.bfloat16)
    frames, select, keep, conv_weight = lax.optimization_barrier((frames, select, keep, conv_weight))
    rimmed = with_halo(frames, (("seq", 2),), 1)[0]
    conv = causal_conv(rimmed, conv_weight, keep)
    cells = (frames[0].astype(jnp.float32) + jax.nn.silu(conv)).astype(jnp.bfloat16)
    tokens = lax.conv_general_dilated(
        cells,
        w_latent.reshape(4, 4, chans, LAT),
        (4, 4),
        "VALID",
        dimension_numbers=("NHWC", "HWIO", "NHWC"),
        preferred_element_type=jnp.float32,
    ).astype(jnp.bfloat16)
    latent_out = tokens.reshape(1, nframes, tok_rows, tok_cols * LAT)
    tokens = tokens.reshape(-1, LAT)
    tok_clip = jnp.repeat(clip_of, tok_rows * tok_cols).astype(jnp.float32) + 1.0
    outgoing = (
        jnp.dot(select, tokens, preferred_element_type=jnp.float32)
        .astype(jnp.bfloat16)
        .reshape(nseq, capacity, LAT)
    )
    labels = (
        jnp.dot(select, tok_clip.astype(jnp.bfloat16)[:, None], preferred_element_type=jnp.float32)
        .astype(jnp.bfloat16)
        .reshape(nseq, 1, capacity)
    )
    labels = jnp.pad(labels, ((0, 0), (0, 0), (0, LAT - capacity)))
    arrived = lax.all_to_all(
        jnp.concatenate([outgoing, labels], axis=1), "seq", split_axis=0, concat_axis=0, tiled=True
    )
    x0 = arrived[:, :capacity].reshape(slots, LAT).astype(jnp.float32)
    tag = arrived[:, capacity, :capacity].reshape(slots).astype(jnp.float32)
    kind = clip_group[0].astype(jnp.float32)
    coef = (
        (2.0 * kind - 1.0)
        * (0.1 + timesteps[0].astype(jnp.float32) / 1000.0)
        / (counts.astype(jnp.float32) * per_frame)
    )
    slot_hot = (tag[:, None] == (jnp.arange(CLIPS, dtype=jnp.float32) + 1.0)[None, :]).astype(
        jnp.float32
    )
    slot_coef = jnp.sum(slot_hot * coef[None, :], axis=1)
    slot_kind = jnp.sum(slot_hot * kind[None, :], axis=1)
    states = hidden[0].astype(jnp.float32)
    mean = jnp.mean(states, axis=1, keepdims=True)
    centred = states - mean
    var = jnp.mean(centred * centred, axis=1, keepdims=True)
    normed = (centred * lax.rsqrt(var + 1e-06)).astype(jnp.bfloat16)
    pred = jnp.dot(normed, w_out, preferred_element_type=jnp.float32)
    target = slot_kind[:, None] * teacher[0] + (1.0 - slot_kind[:, None]) * (noise[0] - x0)
    diff = pred - target
    err = jnp.sum(diff * diff, axis=1)
    partial_loss = coef * jnp.sum(slot_hot * err[:, None], axis=0)
    dpred = (2.0 * slot_coef[:, None] * diff).astype(jnp.bfloat16)
    states_t = hidden[0].T.astype(jnp.float32)
    normed_t = ((states_t - mean.T) * lax.rsqrt(var.T + 1e-06)).astype(jnp.bfloat16)
    grad_t = lax.dot_general(
        dpred, normed_t, (((0,), (1,)), ((), ())), preferred_element_type=jnp.float32
    )
    ndp = lax.axis_size("dp")
    share = grad_t.shape[1] // nseq
    lanes = 128
    dense = LAT * share // lanes
    assert ndp * CLIPS <= lanes and dense * lanes == LAT * share
    place = lax.axis_index("dp") * CLIPS
    loss_row = lax.dynamic_update_slice(jnp.zeros((lanes,), jnp.float32), partial_loss, (place,))
    summed = tree_reduce(grad_t, loss_row, nseq, ndp)
    grad_mine = summed[:dense].reshape(LAT, share).T
    clip_loss = lax.dynamic_slice_in_dim(summed[dense], place, CLIPS).reshape(1, CLIPS)
    return (latent_out, clip_loss, grad_mine)


def solution(mesh):
    return jax.shard_map(
        per_device,
        mesh=mesh,
        in_specs=(
            P("dp", None, "seq", None, None),
            P("dp", None),
            P("dp", None),
            P("dp", None),
            P("dp", "seq", None, None),
            P(),
            P(),
            P("dp", "seq", None),
            P("dp", "seq", None),
            P("dp", "seq", None),
            P(),
        ),
        out_specs=(P("dp", None, "seq", None), P("dp", None), P("seq", None)),
        check_vma=False,
    )
```

```python
import jax
import jax.numpy as jnp
from jax import lax
from jax.sharding import PartitionSpec as P

LAT = 64
CLIPS = 4


def with_halo(cells, sides, width):
    for axis, dim in sides:
        count = lax.axis_size(axis)
        ends = count - 1
        head = lax.slice_in_dim(cells, 0, width, axis=dim)
        tail = lax.slice_in_dim(cells, cells.shape[dim] - width, cells.shape[dim], axis=dim)
        cells = jnp.concatenate(
            [
                lax.ppermute(tail, axis, [(i, (i + 1) % count) for i in range(ends)]),
                cells,
                lax.ppermute(head, axis, [((i + 1) % count, i) for i in range(ends)]),
            ],
            axis=dim,
        )
    return cells


def causal_conv(rimmed, conv_weight, keep):
    nframes = rimmed.shape[0]
    chans = rimmed.shape[-1]
    padded = jnp.pad(rimmed, ((0, 0), (0, 0), (1, 1), (0, 0)))
    kernel = jnp.transpose(conv_weight, (1, 2, 3, 0, 4)).reshape(3, 3, chans, 3 * chans)
    each = lax.conv_general_dilated(
        padded,
        kernel,
        (1, 1),
        "VALID",
        dimension_numbers=("NHWC", "HWIO", "NHWC"),
        preferred_element_type=jnp.float32,
    )
    total = each[..., :chans]
    for lag in (1, 2):
        part = each[: nframes - lag, ..., lag * chans : (lag + 1) * chans]
        part = jnp.pad(part, ((lag, 0), (0, 0), (0, 0), (0, 0)))
        total = total + part * keep[lag][:, None, None, None]
    return total


def tree_reduce(grad_t, loss_row, nseq, ndp):
    nbits = nseq.bit_length() - 1
    assert nbits >= 1 and 1 << nbits == nseq and ndp & (ndp - 1) == 0
    groups = [2] + [1] * (nbits - 3) if nbits >= 3 else [1] * (nbits - 1)
    lat, _, _, share = grad_t.shape
    lanes = loss_row.shape[0]
    dense = lat * share // lanes
    me = lax.axis_index("seq")
    halves = grad_t
    loss_rows = jnp.broadcast_to(loss_row[None, None, :], (nseq // 2, 1, lanes))

    def half(bit):
        part = lax.dynamic_index_in_dim(halves, bit, 2, keepdims=False)
        part = part.transpose(1, 0, 2).reshape(nseq // 2, dense, lanes)
        return jnp.concatenate([part, loss_rows], axis=1)

    bit = me & 1
    x = half(bit) + lax.ppermute(half(1 - bit), "seq", [(i, i ^ 1) for i in range(nseq)])
    tail = x.shape[1:]
    low = 1
    for width in groups:
        ways = 1 << width
        x = x.reshape((x.shape[0] // ways, ways) + tail)
        digit = (me >> low) & (ways - 1)
        total = lax.dynamic_index_in_dim(x, digit, 1, keepdims=False)
        for step in range(1, ways):
            send = lax.dynamic_index_in_dim(x, digit ^ step, 1, keepdims=False)
            pairs = [(i, i ^ (step << low)) for i in range(nseq)]
            total = total + lax.ppermute(send, "seq", pairs)
        x = total
        low += width
    x = x.reshape(tail)
    for k in range(ndp.bit_length() - 1):
        x = x + lax.ppermute(x, "dp", [(i, i ^ (1 << k)) for i in range(ndp)])
    return x


def per_device(
    frames,
    frame_counts,
    clip_group,
    timesteps,
    owner_map,
    conv_weight,
    w_latent,
    hidden,
    noise,
    teacher,
    w_out,
):
    nseq = lax.axis_size("seq")
    local = frames[0]
    nframes, nrows, width, chans = local.shape
    tok_rows = nrows // 4
    tok_cols = width // 4
    per_frame = nrows * nseq // 4 * tok_cols
    counts = frame_counts[0]
    ends = jnp.cumsum(counts)
    index = jnp.arange(nframes, dtype=jnp.int32)
    clip_of = jnp.sum((index[:, None] >= ends[None, :]).astype(jnp.int32), axis=1)
    clip_hot = (clip_of[:, None] == jnp.arange(CLIPS, dtype=jnp.int32)[None, :]).astype(jnp.int32)
    starts = jnp.sum(clip_hot * (ends - counts)[None, :], axis=1)
    keep = jnp.stack([(index - lag >= starts).astype(jnp.float32) for lag in range(3)])
    rimmed = with_halo(frames, (("seq", 2),), 1)[0]
    conv = causal_conv(rimmed, conv_weight, keep)
    cells = (local.astype(jnp.float32) + jax.nn.silu(conv)).astype(jnp.bfloat16)
    tokens = lax.conv_general_dilated(
        cells,
        w_latent.reshape(4, 4, chans, LAT),
        (4, 4),
        "VALID",
        dimension_numbers=("NHWC", "HWIO", "NHWC"),
        preferred_element_type=jnp.float32,
    ).astype(jnp.bfloat16)
    latent_out = tokens.reshape(1, nframes, tok_rows, tok_cols * LAT)
    tokens = tokens.reshape(-1, LAT)
    slots = hidden.shape[1]
    capacity = slots // nseq
    assert capacity <= LAT
    owners = owner_map.reshape(-1)
    owner_hot = (owners[:, None] == jnp.arange(nseq, dtype=jnp.int32)[None, :]).astype(jnp.int32)
    ntok = owners.shape[0]
    upto = (jnp.arange(ntok)[:, None] >= jnp.arange(ntok)[None, :]).astype(jnp.bfloat16)
    running = jnp.dot(upto, owner_hot.astype(jnp.bfloat16), preferred_element_type=jnp.float32)
    rank = jnp.sum(running * owner_hot.astype(jnp.float32), axis=1).astype(jnp.int32) - 1
    dest = owners * capacity + rank
    select = (dest[None, :] == jnp.arange(slots, dtype=jnp.int32)[:, None]).astype(jnp.bfloat16)
    tok_clip = jnp.repeat(clip_of, tok_rows * tok_cols).astype(jnp.float32) + 1.0
    outgoing = (
        jnp.dot(select, tokens, preferred_element_type=jnp.float32)
        .astype(jnp.bfloat16)
        .reshape(nseq, capacity, LAT)
    )
    labels = (
        jnp.dot(select, tok_clip.astype(jnp.bfloat16)[:, None], preferred_element_type=jnp.float32)
        .astype(jnp.bfloat16)
        .reshape(nseq, 1, capacity)
    )
    labels = jnp.pad(labels, ((0, 0), (0, 0), (0, LAT - capacity)))
    arrived = lax.all_to_all(
        jnp.concatenate([outgoing, labels], axis=1), "seq", split_axis=0, concat_axis=0, tiled=True
    )
    x0 = arrived[:, :capacity].reshape(slots, LAT).astype(jnp.float32)
    tag = arrived[:, capacity, :capacity].reshape(slots).astype(jnp.float32)
    kind = clip_group[0].astype(jnp.float32)
    coef = (
        (2.0 * kind - 1.0)
        * (0.1 + timesteps[0].astype(jnp.float32) / 1000.0)
        / (counts.astype(jnp.float32) * per_frame)
    )
    slot_hot = (tag[:, None] == (jnp.arange(CLIPS, dtype=jnp.float32) + 1.0)[None, :]).astype(
        jnp.float32
    )
    slot_coef = jnp.sum(slot_hot * coef[None, :], axis=1)
    slot_kind = jnp.sum(slot_hot * kind[None, :], axis=1)
    states = hidden[0].astype(jnp.float32)
    mean = jnp.mean(states, axis=1, keepdims=True)
    centred = states - mean
    var = jnp.mean(centred * centred, axis=1, keepdims=True)
    normed = (centred * lax.rsqrt(var + 1e-06)).astype(jnp.bfloat16)
    pred = jnp.dot(normed, w_out, preferred_element_type=jnp.float32)
    target = slot_kind[:, None] * teacher[0] + (1.0 - slot_kind[:, None]) * (noise[0] - x0)
    diff = pred - target
    err = jnp.sum(diff * diff, axis=1)
    partial_loss = coef * jnp.sum(slot_hot * err[:, None], axis=0)
    dpred = (2.0 * slot_coef[:, None] * diff).astype(jnp.bfloat16)
    states_t = hidden[0].T.astype(jnp.float32)
    normed_t = ((states_t - mean.T) * lax.rsqrt(var.T + 1e-06)).astype(jnp.bfloat16)
    share = normed_t.shape[0] // nseq
    grad_t = lax.dot_general(
        dpred,
        normed_t.reshape(nseq // 2, 2, share, slots),
        (((0,), (3,)), ((), ())),
        preferred_element_type=jnp.float32,
    )
    ndp = lax.axis_size("dp")
    lanes = 128
    dense = LAT * share // lanes
    assert ndp * CLIPS <= lanes and dense * lanes == LAT * share
    place = lax.axis_index("dp") * CLIPS
    loss_row = lax.dynamic_update_slice(jnp.zeros((lanes,), jnp.float32), partial_loss, (place,))
    summed = tree_reduce(grad_t, loss_row, nseq, ndp)
    grad_mine = summed[:dense].reshape(LAT, share).T
    clip_loss = lax.dynamic_slice_in_dim(summed[dense], place, CLIPS).reshape(1, CLIPS)
    return (latent_out, clip_loss, grad_mine)


def solution(mesh):
    return jax.shard_map(
        per_device,
        mesh=mesh,
        in_specs=(
            P("dp", None, "seq", None, None),
            P("dp", None),
            P("dp", None),
            P("dp", None),
            P("dp", "seq", None, None),
            P(),
            P(),
            P("dp", "seq", None),
            P("dp", "seq", None),
            P("dp", "seq", None),
            P(),
        ),
        out_specs=(P("dp", None, "seq", None), P("dp", None), P("seq", None)),
        check_vma=False,
    )
```

```python
import jax
import jax.numpy as jnp
from jax import lax
from jax.sharding import PartitionSpec as P

LAT = 64
CLIPS = 4


def with_halo(cells, sides, width):
    for axis, dim in sides:
        count = lax.axis_size(axis)
        ends = count - 1
        head = lax.slice_in_dim(cells, 0, width, axis=dim)
        tail = lax.slice_in_dim(cells, cells.shape[dim] - width, cells.shape[dim], axis=dim)
        cells = jnp.concatenate(
            [
                lax.ppermute(tail, axis, [(i, (i + 1) % count) for i in range(ends)]),
                cells,
                lax.ppermute(head, axis, [((i + 1) % count, i) for i in range(ends)]),
            ],
            axis=dim,
        )
    return cells


def causal_conv(rimmed, conv_weight, keep):
    nframes = rimmed.shape[0]
    chans = rimmed.shape[-1]
    padded = jnp.pad(rimmed, ((0, 0), (0, 0), (1, 1), (0, 0)))
    kernel = jnp.transpose(conv_weight, (1, 2, 3, 0, 4)).reshape(3, 3, chans, 3 * chans)
    each = lax.conv_general_dilated(
        padded,
        kernel,
        (1, 1),
        "VALID",
        dimension_numbers=("NHWC", "HWIO", "NHWC"),
        preferred_element_type=jnp.float32,
    )
    total = each[..., :chans]
    for lag in (1, 2):
        part = each[: nframes - lag, ..., lag * chans : (lag + 1) * chans]
        part = jnp.pad(part, ((lag, 0), (0, 0), (0, 0), (0, 0)))
        total = total + part * keep[lag][:, None, None, None]
    return total


def tree_reduce(grad_t, loss_row, nseq, ndp):
    nbits = nseq.bit_length() - 1
    assert nbits >= 1 and 1 << nbits == nseq and ndp & (ndp - 1) == 0
    groups = [2] + [1] * (nbits - 3) if nbits >= 3 else [1] * (nbits - 1)
    lat = grad_t.shape[0]
    share = grad_t.shape[1] // nseq
    lanes = loss_row.shape[0]
    dense = lat * share // lanes
    me = lax.axis_index("seq")
    halves = grad_t.reshape(lat, nseq // 2, 2, share)
    loss_rows = jnp.broadcast_to(loss_row[None, None, :], (nseq // 2, 1, lanes))

    def half(bit):
        part = lax.dynamic_index_in_dim(halves, bit, 2, keepdims=False)
        part = part.transpose(1, 0, 2).reshape(nseq // 2, dense, lanes)
        return jnp.concatenate([part, loss_rows], axis=1)

    bit = me & 1
    x = half(bit) + lax.ppermute(half(1 - bit), "seq", [(i, i ^ 1) for i in range(nseq)])
    tail = x.shape[1:]
    low = 1
    for width in groups:
        ways = 1 << width
        x = x.reshape((x.shape[0] // ways, ways) + tail)
        digit = (me >> low) & (ways - 1)
        total = lax.dynamic_index_in_dim(x, digit, 1, keepdims=False)
        for step in range(1, ways):
            send = lax.dynamic_index_in_dim(x, digit ^ step, 1, keepdims=False)
            pairs = [(i, i ^ (step << low)) for i in range(nseq)]
            total = total + lax.ppermute(send, "seq", pairs)
        x = total
        low += width
    x = x.reshape(tail)
    for k in range(ndp.bit_length() - 1):
        x = x + lax.ppermute(x, "dp", [(i, i ^ (1 << k)) for i in range(ndp)])
    return x


def per_device(
    frames,
    frame_counts,
    clip_group,
    timesteps,
    owner_map,
    conv_weight,
    w_latent,
    hidden,
    noise,
    teacher,
    w_out,
):
    nseq = lax.axis_size("seq")
    local = frames[0]
    nframes, nrows, width, chans = local.shape
    tok_rows = nrows // 4
    tok_cols = width // 4
    per_frame = nrows * nseq // 4 * tok_cols
    counts = frame_counts[0]
    ends = jnp.cumsum(counts)
    index = jnp.arange(nframes, dtype=jnp.int32)
    clip_of = jnp.sum((index[:, None] >= ends[None, :]).astype(jnp.int32), axis=1)
    clip_hot = (clip_of[:, None] == jnp.arange(CLIPS, dtype=jnp.int32)[None, :]).astype(jnp.int32)
    starts = jnp.sum(clip_hot * (ends - counts)[None, :], axis=1)
    keep = jnp.stack([(index - lag >= starts).astype(jnp.float32) for lag in range(3)])
    rimmed = with_halo(frames, (("seq", 2),), 1)[0]
    conv = causal_conv(rimmed, conv_weight, keep)
    cells = (local.astype(jnp.float32) + jax.nn.silu(conv)).astype(jnp.bfloat16)
    tokens = lax.conv_general_dilated(
        cells,
        w_latent.reshape(4, 4, chans, LAT),
        (4, 4),
        "VALID",
        dimension_numbers=("NHWC", "HWIO", "NHWC"),
        preferred_element_type=jnp.float32,
    ).astype(jnp.bfloat16)
    latent_out = tokens.reshape(1, nframes, tok_rows, tok_cols * LAT)
    tokens = tokens.reshape(-1, LAT)
    slots = hidden.shape[1]
    capacity = slots // nseq
    assert capacity <= LAT
    owners = owner_map.reshape(-1)
    owner_hot = (owners[:, None] == jnp.arange(nseq, dtype=jnp.int32)[None, :]).astype(jnp.int32)
    ntok = owners.shape[0]
    upto = (jnp.arange(ntok)[:, None] >= jnp.arange(ntok)[None, :]).astype(jnp.bfloat16)
    running = jnp.dot(upto, owner_hot.astype(jnp.bfloat16), preferred_element_type=jnp.float32)
    rank = jnp.sum(running * owner_hot.astype(jnp.float32), axis=1).astype(jnp.int32) - 1
    dest = owners * capacity + rank
    select = (dest[None, :] == jnp.arange(slots, dtype=jnp.int32)[:, None]).astype(jnp.bfloat16)
    tok_clip = jnp.repeat(clip_of, tok_rows * tok_cols).astype(jnp.float32) + 1.0
    outgoing = (
        jnp.dot(select, tokens, preferred_element_type=jnp.float32)
        .astype(jnp.bfloat16)
        .reshape(nseq, capacity, LAT)
    )
    labels = (
        jnp.dot(select, tok_clip.astype(jnp.bfloat16)[:, None], preferred_element_type=jnp.float32)
        .astype(jnp.bfloat16)
        .reshape(nseq, 1, capacity)
    )
    labels = jnp.pad(labels, ((0, 0), (0, 0), (0, LAT - capacity)))
    arrived = lax.all_to_all(
        jnp.concatenate([outgoing, labels], axis=1), "seq", split_axis=0, concat_axis=0, tiled=True
    )
    x0 = arrived[:, :capacity].reshape(slots, LAT).astype(jnp.float32)
    tag = arrived[:, capacity, :capacity].reshape(slots).astype(jnp.float32)
    kind = clip_group[0].astype(jnp.float32)
    coef = (
        (2.0 * kind - 1.0)
        * (0.1 + timesteps[0].astype(jnp.float32) / 1000.0)
        / (counts.astype(jnp.float32) * per_frame)
    )
    slot_hot = (tag[:, None] == (jnp.arange(CLIPS, dtype=jnp.float32) + 1.0)[None, :]).astype(
        jnp.float32
    )
    slot_coef = jnp.sum(slot_hot * coef[None, :], axis=1)
    slot_kind = jnp.sum(slot_hot * kind[None, :], axis=1)
    states = hidden[0].astype(jnp.float32)
    mean = jnp.mean(states, axis=1, keepdims=True)
    centred = states - mean
    var = jnp.mean(centred * centred, axis=1, keepdims=True)
    normed = (centred * lax.rsqrt(var + 1e-06)).astype(jnp.bfloat16)
    pred = jnp.dot(normed, w_out, preferred_element_type=jnp.float32)
    target = slot_kind[:, None] * teacher[0] + (1.0 - slot_kind[:, None]) * (noise[0] - x0)
    diff = pred - target
    err = jnp.sum(diff * diff, axis=1)
    partial_loss = coef * jnp.sum(slot_hot * err[:, None], axis=0)
    dpred = (2.0 * slot_coef[:, None] * diff).astype(jnp.bfloat16)
    states_t = hidden[0].T.astype(jnp.float32)
    normed_t = ((states_t - mean.T) * lax.rsqrt(var.T + 1e-06)).astype(jnp.bfloat16)
    grad_t = lax.dot_general(
        dpred, normed_t, (((0,), (1,)), ((), ())), preferred_element_type=jnp.float32
    )
    ndp = lax.axis_size("dp")
    share = grad_t.shape[1] // nseq
    lanes = 128
    dense = LAT * share // lanes
    assert ndp * CLIPS <= lanes and dense * lanes == LAT * share
    place = lax.axis_index("dp") * CLIPS
    loss_row = lax.dynamic_update_slice(jnp.zeros((lanes,), jnp.float32), partial_loss, (place,))
    summed = tree_reduce(grad_t, loss_row, nseq, ndp)
    grad_mine = summed[:dense].reshape(LAT, share).T
    clip_loss = lax.dynamic_slice_in_dim(summed[dense], place, CLIPS).reshape(1, CLIPS)
    return (latent_out, clip_loss, grad_mine)


def solution(mesh):
    return jax.shard_map(
        per_device,
        mesh=mesh,
        in_specs=(
            P("dp", None, "seq", None, None),
            P("dp", None),
            P("dp", None),
            P("dp", None),
            P("dp", "seq", None, None),
            P(),
            P(),
            P("dp", "seq", None),
            P("dp", "seq", None),
            P("dp", "seq", None),
            P(),
        ),
        out_specs=(P("dp", None, "seq", None), P("dp", None), P("seq", None)),
        check_vma=False,
    )
```

```python
import jax
import jax.numpy as jnp
from jax import lax
from jax.sharding import PartitionSpec as P

LAT = 64
CLIPS = 4


def with_halo(cells, sides, width):
    for axis, dim in sides:
        count = lax.axis_size(axis)
        ends = count - 1
        head = lax.slice_in_dim(cells, 0, width, axis=dim)
        tail = lax.slice_in_dim(cells, cells.shape[dim] - width, cells.shape[dim], axis=dim)
        cells = jnp.concatenate(
            [
                lax.ppermute(tail, axis, [(i, (i + 1) % count) for i in range(ends)]),
                cells,
                lax.ppermute(head, axis, [((i + 1) % count, i) for i in range(ends)]),
            ],
            axis=dim,
        )
    return cells


def causal_conv(rimmed, conv_weight, keep):
    nframes = rimmed.shape[0]
    chans = rimmed.shape[-1]
    padded = jnp.pad(rimmed, ((0, 0), (0, 0), (1, 1), (0, 0)))
    kernel = jnp.transpose(conv_weight, (1, 2, 3, 0, 4)).reshape(3, 3, chans, 3 * chans)
    each = lax.conv_general_dilated(
        padded,
        kernel,
        (1, 1),
        "VALID",
        dimension_numbers=("NHWC", "HWIO", "NHWC"),
        preferred_element_type=jnp.float32,
    )
    total = each[..., :chans]
    for lag in (1, 2):
        part = each[: nframes - lag, ..., lag * chans : (lag + 1) * chans]
        part = jnp.pad(part, ((lag, 0), (0, 0), (0, 0), (0, 0)))
        total = total + part * keep[lag][:, None, None, None]
    return total


def tree_reduce(grad_t, loss_line, nseq, ndp):
    nbits = nseq.bit_length() - 1
    assert nbits >= 1 and 1 << nbits == nseq and ndp & (ndp - 1) == 0
    groups = [2] + [1] * (nbits - 3) if nbits >= 3 else [1] * (nbits - 1)
    lat = grad_t.shape[0]
    share = grad_t.shape[1] // nseq
    lanes = 128
    dense = lat * share // lanes
    me = lax.axis_index("seq")
    x = jnp.concatenate([grad_t, loss_line[None, :]], axis=0).reshape(lat + 1, nseq // 2, 2, share)
    bit = me & 1
    keep = lax.dynamic_index_in_dim(x, bit, 2, keepdims=False)
    send = lax.dynamic_index_in_dim(x, 1 - bit, 2, keepdims=False)
    x = keep + lax.ppermute(send, "seq", [(i, i ^ 1) for i in range(nseq)])
    body = x[:lat].transpose(1, 0, 2).reshape(nseq // 2, dense, lanes)
    loss_rows = x[lat, :, : min(share, lanes)]
    loss_rows = jnp.pad(loss_rows, ((0, 0), (0, lanes - loss_rows.shape[1])))[:, None, :]
    x = jnp.concatenate([body, loss_rows], axis=1)
    tail = x.shape[1:]
    low = 1
    for width in groups:
        ways = 1 << width
        x = x.reshape((x.shape[0] // ways, ways) + tail)
        digit = (me >> low) & (ways - 1)
        total = lax.dynamic_index_in_dim(x, digit, 1, keepdims=False)
        for step in range(1, ways):
            send = lax.dynamic_index_in_dim(x, digit ^ step, 1, keepdims=False)
            pairs = [(i, i ^ (step << low)) for i in range(nseq)]
            total = total + lax.ppermute(send, "seq", pairs)
        x = total
        low += width
    x = x.reshape(tail)
    for k in range(ndp.bit_length() - 1):
        x = x + lax.ppermute(x, "dp", [(i, i ^ (1 << k)) for i in range(ndp)])
    return x


def per_device(
    frames,
    frame_counts,
    clip_group,
    timesteps,
    owner_map,
    conv_weight,
    w_latent,
    hidden,
    noise,
    teacher,
    w_out,
):
    nseq = lax.axis_size("seq")
    local = frames[0]
    nframes, nrows, width, chans = local.shape
    tok_rows = nrows // 4
    tok_cols = width // 4
    per_frame = nrows * nseq // 4 * tok_cols
    counts = frame_counts[0]
    ends = jnp.cumsum(counts)
    index = jnp.arange(nframes, dtype=jnp.int32)
    clip_of = jnp.sum((index[:, None] >= ends[None, :]).astype(jnp.int32), axis=1)
    clip_hot = (clip_of[:, None] == jnp.arange(CLIPS, dtype=jnp.int32)[None, :]).astype(jnp.int32)
    starts = jnp.sum(clip_hot * (ends - counts)[None, :], axis=1)
    keep = jnp.stack([(index - lag >= starts).astype(jnp.float32) for lag in range(3)])
    rimmed = with_halo(frames, (("seq", 2),), 1)[0]
    conv = causal_conv(rimmed, conv_weight, keep)
    cells = (local.astype(jnp.float32) + jax.nn.silu(conv)).astype(jnp.bfloat16)
    tokens = lax.conv_general_dilated(
        cells,
        w_latent.reshape(4, 4, chans, LAT),
        (4, 4),
        "VALID",
        dimension_numbers=("NHWC", "HWIO", "NHWC"),
        preferred_element_type=jnp.float32,
    ).astype(jnp.bfloat16)
    latent_out = tokens.reshape(1, nframes, tok_rows, tok_cols * LAT)
    tokens = tokens.reshape(-1, LAT)
    slots = hidden.shape[1]
    capacity = slots // nseq
    assert capacity <= LAT
    owners = owner_map.reshape(-1)
    owner_hot = (owners[:, None] == jnp.arange(nseq, dtype=jnp.int32)[None, :]).astype(jnp.int32)
    ntok = owners.shape[0]
    upto = (jnp.arange(ntok)[:, None] >= jnp.arange(ntok)[None, :]).astype(jnp.bfloat16)
    running = jnp.dot(upto, owner_hot.astype(jnp.bfloat16), preferred_element_type=jnp.float32)
    rank = jnp.sum(running * owner_hot.astype(jnp.float32), axis=1).astype(jnp.int32) - 1
    dest = owners * capacity + rank
    select = (dest[None, :] == jnp.arange(slots, dtype=jnp.int32)[:, None]).astype(jnp.bfloat16)
    tok_clip = jnp.repeat(clip_of, tok_rows * tok_cols).astype(jnp.float32) + 1.0
    outgoing = (
        jnp.dot(select, tokens, preferred_element_type=jnp.float32)
        .astype(jnp.bfloat16)
        .reshape(nseq, capacity, LAT)
    )
    labels = (
        jnp.dot(select, tok_clip.astype(jnp.bfloat16)[:, None], preferred_element_type=jnp.float32)
        .astype(jnp.bfloat16)
        .reshape(nseq, 1, capacity)
    )
    labels = jnp.pad(labels, ((0, 0), (0, 0), (0, LAT - capacity)))
    arrived = lax.all_to_all(
        jnp.concatenate([outgoing, labels], axis=1), "seq", split_axis=0, concat_axis=0, tiled=True
    )
    x0 = arrived[:, :capacity].reshape(slots, LAT).astype(jnp.float32)
    tag = arrived[:, capacity, :capacity].reshape(slots).astype(jnp.float32)
    kind = clip_group[0].astype(jnp.float32)
    coef = (
        (2.0 * kind - 1.0)
        * (0.1 + timesteps[0].astype(jnp.float32) / 1000.0)
        / (counts.astype(jnp.float32) * per_frame)
    )
    slot_hot = (tag[:, None] == (jnp.arange(CLIPS, dtype=jnp.float32) + 1.0)[None, :]).astype(
        jnp.float32
    )
    slot_coef = jnp.sum(slot_hot * coef[None, :], axis=1)
    slot_kind = jnp.sum(slot_hot * kind[None, :], axis=1)
    states = hidden[0].astype(jnp.float32)
    mean = jnp.mean(states, axis=1, keepdims=True)
    centred = states - mean
    var = jnp.mean(centred * centred, axis=1, keepdims=True)
    normed = (centred * lax.rsqrt(var + 1e-06)).astype(jnp.bfloat16)
    pred = jnp.dot(normed, w_out, preferred_element_type=jnp.float32)
    target = slot_kind[:, None] * teacher[0] + (1.0 - slot_kind[:, None]) * (noise[0] - x0)
    diff = pred - target
    err = jnp.sum(diff * diff, axis=1)
    partial_loss = coef * jnp.sum(slot_hot * err[:, None], axis=0)
    dpred = (2.0 * slot_coef[:, None] * diff).astype(jnp.bfloat16)
    states_t = hidden[0].T.astype(jnp.float32)
    normed_t = ((states_t - mean.T) * lax.rsqrt(var.T + 1e-06)).astype(jnp.bfloat16)
    grad_t = lax.dot_general(
        dpred, normed_t, (((0,), (1,)), ((), ())), preferred_element_type=jnp.float32
    )
    ndp = lax.axis_size("dp")
    share = grad_t.shape[1] // nseq
    dense = LAT * share // 128
    assert ndp * CLIPS <= min(share, 128) and dense * 128 == LAT * share
    place = lax.axis_index("dp") * CLIPS
    loss_row = lax.dynamic_update_slice(jnp.zeros((share,), jnp.float32), partial_loss, (place,))
    summed = tree_reduce(grad_t, jnp.tile(loss_row, nseq), nseq, ndp)
    grad_mine = summed[:dense].reshape(LAT, share).T
    clip_loss = lax.dynamic_slice_in_dim(summed[dense], place, CLIPS).reshape(1, CLIPS)
    return (latent_out, clip_loss, grad_mine)


def solution(mesh):
    return jax.shard_map(
        per_device,
        mesh=mesh,
        in_specs=(
            P("dp", None, "seq", None, None),
            P("dp", None),
            P("dp", None),
            P("dp", None),
            P("dp", "seq", None, None),
            P(),
            P(),
            P("dp", "seq", None),
            P("dp", "seq", None),
            P("dp", "seq", None),
            P(),
        ),
        out_specs=(P("dp", None, "seq", None), P("dp", None), P("seq", None)),
        check_vma=False,
    )
```

```python
import jax
import jax.numpy as jnp
from jax import lax
from jax.experimental import pallas as pl
from jax.experimental.pallas import tpu as pltpu
from jax.sharding import PartitionSpec as P

LAT = 64
CLIPS = 4


def _conv_kernel(keep_ref, frames_ref, top_ref, bottom_ref, w_ref, cells_ref):
    nframes, nrows, width, chans = frames_ref.shape
    col = lax.broadcasted_iota(jnp.int32, (nrows + 2, width, chans), 1)

    def slab(g):
        x = jnp.concatenate([top_ref[g], frames_ref[g], bottom_ref[g]], axis=0).astype(jnp.float32)
        left = jnp.where(col == 0, 0.0, pltpu.roll(x, 1, 1))
        right = jnp.where(col == width - 1, 0.0, pltpu.roll(x, width - 1, 1))
        return jnp.concatenate([left, x, right], axis=-1).astype(jnp.bfloat16)

    def body(f, carry):
        acc = jnp.zeros((nrows * width, chans), jnp.float32)
        for lag in range(3):
            g = jnp.maximum(f - lag, 0)
            wide = slab(g)
            part = jnp.zeros((nrows * width, chans), jnp.float32)
            for i in range(3):
                rows = wide[i : i + nrows].reshape(nrows * width, 3 * chans)
                part = part + jnp.dot(rows, w_ref[lag, i], preferred_element_type=jnp.float32)
            acc = acc + part * keep_ref[lag, f]
        conv = acc.reshape(nrows, width, chans)
        out = frames_ref[f].astype(jnp.float32) + conv * jax.nn.sigmoid(conv)
        cells_ref[f] = out.astype(cells_ref.dtype)
        return carry

    lax.fori_loop(0, nframes, body, 0)


def conv_cells(keep, local, top, bottom, conv_weight):
    nframes, nrows, width, chans = local.shape
    w = conv_weight.reshape(3, 3, 3 * chans, chans)
    vmem = pltpu.VMEM
    return pl.pallas_call(
        _conv_kernel,
        out_shape=jax.ShapeDtypeStruct(local.shape, jnp.bfloat16),
        in_specs=[pl.BlockSpec(memory_space=pltpu.SMEM)] + [pl.BlockSpec(memory_space=vmem)] * 4,
        out_specs=pl.BlockSpec(memory_space=vmem),
        cost_estimate=pl.CostEstimate(
            flops=2 * 27 * nframes * nrows * width * chans * chans,
            bytes_accessed=2 * (2 * local.size + top.size + bottom.size + conv_weight.size),
            transcendentals=nframes * nrows * width * chans,
        ),
    )(keep, local, top, bottom, w)


def tree_reduce(grad_t, loss_row, nseq, ndp):
    nbits = nseq.bit_length() - 1
    assert nbits >= 1 and 1 << nbits == nseq and ndp & (ndp - 1) == 0
    groups = [2] + [1] * (nbits - 3) if nbits >= 3 else [1] * (nbits - 1)
    lat = grad_t.shape[0]
    share = grad_t.shape[1] // nseq
    lanes = loss_row.shape[0]
    dense = lat * share // lanes
    me = lax.axis_index("seq")
    halves = grad_t.reshape(lat, nseq // 2, 2, share)
    loss_rows = jnp.broadcast_to(loss_row[None, None, :], (nseq // 2, 1, lanes))

    def half(bit):
        part = lax.dynamic_index_in_dim(halves, bit, 2, keepdims=False)
        part = part.transpose(1, 0, 2).reshape(nseq // 2, dense, lanes)
        return jnp.concatenate([part, loss_rows], axis=1)

    bit = me & 1
    x = half(bit) + lax.ppermute(half(1 - bit), "seq", [(i, i ^ 1) for i in range(nseq)])
    tail = x.shape[1:]
    low = 1
    for width in groups:
        ways = 1 << width
        x = x.reshape((x.shape[0] // ways, ways) + tail)
        digit = (me >> low) & (ways - 1)
        total = lax.dynamic_index_in_dim(x, digit, 1, keepdims=False)
        for step in range(1, ways):
            send = lax.dynamic_index_in_dim(x, digit ^ step, 1, keepdims=False)
            pairs = [(i, i ^ (step << low)) for i in range(nseq)]
            total = total + lax.ppermute(send, "seq", pairs)
        x = total
        low += width
    x = x.reshape(tail)
    for k in range(ndp.bit_length() - 1):
        x = x + lax.ppermute(x, "dp", [(i, i ^ (1 << k)) for i in range(ndp)])
    return x


def per_device(
    frames,
    frame_counts,
    clip_group,
    timesteps,
    owner_map,
    conv_weight,
    w_latent,
    hidden,
    noise,
    teacher,
    w_out,
):
    nseq = lax.axis_size("seq")
    local = frames[0]
    nframes, nrows, width, chans = local.shape
    tok_rows = nrows // 4
    tok_cols = width // 4
    per_frame = nrows * nseq // 4 * tok_cols
    counts = frame_counts[0]
    ends = jnp.cumsum(counts)
    index = jnp.arange(nframes, dtype=jnp.int32)
    clip_of = jnp.sum((index[:, None] >= ends[None, :]).astype(jnp.int32), axis=1)
    clip_hot = (clip_of[:, None] == jnp.arange(CLIPS, dtype=jnp.int32)[None, :]).astype(jnp.int32)
    starts = jnp.sum(clip_hot * (ends - counts)[None, :], axis=1)
    keep = jnp.stack([(index - lag >= starts).astype(jnp.float32) for lag in range(3)])
    ends_at = nseq - 1
    top = lax.ppermute(local[:, -1:], "seq", [(i, i + 1) for i in range(ends_at)])
    bottom = lax.ppermute(local[:, :1], "seq", [(i + 1, i) for i in range(ends_at)])
    cells = conv_cells(keep, local, top, bottom, conv_weight)
    tokens = lax.conv_general_dilated(
        cells,
        w_latent.reshape(4, 4, chans, LAT),
        (4, 4),
        "VALID",
        dimension_numbers=("NHWC", "HWIO", "NHWC"),
        preferred_element_type=jnp.float32,
    ).astype(jnp.bfloat16)
    latent_out = tokens.reshape(1, nframes, tok_rows, tok_cols * LAT)
    tokens = tokens.reshape(-1, LAT)
    slots = hidden.shape[1]
    capacity = slots // nseq
    assert capacity <= LAT
    owners = owner_map.reshape(-1)
    owner_hot = (owners[:, None] == jnp.arange(nseq, dtype=jnp.int32)[None, :]).astype(jnp.int32)
    ntok = owners.shape[0]
    upto = (jnp.arange(ntok)[:, None] >= jnp.arange(ntok)[None, :]).astype(jnp.bfloat16)
    running = jnp.dot(upto, owner_hot.astype(jnp.bfloat16), preferred_element_type=jnp.float32)
    rank = jnp.sum(running * owner_hot.astype(jnp.float32), axis=1).astype(jnp.int32) - 1
    dest = owners * capacity + rank
    select = (dest[None, :] == jnp.arange(slots, dtype=jnp.int32)[:, None]).astype(jnp.bfloat16)
    tok_clip = jnp.repeat(clip_of, tok_rows * tok_cols).astype(jnp.float32) + 1.0
    outgoing = (
        jnp.dot(select, tokens, preferred_element_type=jnp.float32)
        .astype(jnp.bfloat16)
        .reshape(nseq, capacity, LAT)
    )
    labels = (
        jnp.dot(select, tok_clip.astype(jnp.bfloat16)[:, None], preferred_element_type=jnp.float32)
        .astype(jnp.bfloat16)
        .reshape(nseq, 1, capacity)
    )
    labels = jnp.pad(labels, ((0, 0), (0, 0), (0, LAT - capacity)))
    arrived = lax.all_to_all(
        jnp.concatenate([outgoing, labels], axis=1), "seq", split_axis=0, concat_axis=0, tiled=True
    )
    x0 = arrived[:, :capacity].reshape(slots, LAT).astype(jnp.float32)
    tag = arrived[:, capacity, :capacity].reshape(slots).astype(jnp.float32)
    kind = clip_group[0].astype(jnp.float32)
    coef = (
        (2.0 * kind - 1.0)
        * (0.1 + timesteps[0].astype(jnp.float32) / 1000.0)
        / (counts.astype(jnp.float32) * per_frame)
    )
    slot_hot = (tag[:, None] == (jnp.arange(CLIPS, dtype=jnp.float32) + 1.0)[None, :]).astype(
        jnp.float32
    )
    slot_coef = jnp.sum(slot_hot * coef[None, :], axis=1)
    slot_kind = jnp.sum(slot_hot * kind[None, :], axis=1)
    states = hidden[0].astype(jnp.float32)
    mean = jnp.mean(states, axis=1, keepdims=True)
    centred = states - mean
    var = jnp.mean(centred * centred, axis=1, keepdims=True)
    normed = (centred * lax.rsqrt(var + 1e-06)).astype(jnp.bfloat16)
    pred = jnp.dot(normed, w_out, preferred_element_type=jnp.float32)
    target = slot_kind[:, None] * teacher[0] + (1.0 - slot_kind[:, None]) * (noise[0] - x0)
    diff = pred - target
    err = jnp.sum(diff * diff, axis=1)
    partial_loss = coef * jnp.sum(slot_hot * err[:, None], axis=0)
    dpred = (2.0 * slot_coef[:, None] * diff).astype(jnp.bfloat16)
    states_t = hidden[0].T.astype(jnp.float32)
    normed_t = ((states_t - mean.T) * lax.rsqrt(var.T + 1e-06)).astype(jnp.bfloat16)
    grad_t = lax.dot_general(
        dpred, normed_t, (((0,), (1,)), ((), ())), preferred_element_type=jnp.float32
    )
    ndp = lax.axis_size("dp")
    share = grad_t.shape[1] // nseq
    lanes = 128
    dense = LAT * share // lanes
    assert ndp * CLIPS <= lanes and dense * lanes == LAT * share
    place = lax.axis_index("dp") * CLIPS
    loss_row = lax.dynamic_update_slice(jnp.zeros((lanes,), jnp.float32), partial_loss, (place,))
    summed = tree_reduce(grad_t, loss_row, nseq, ndp)
    grad_mine = summed[:dense].reshape(LAT, share).T
    clip_loss = lax.dynamic_slice_in_dim(summed[dense], place, CLIPS).reshape(1, CLIPS)
    return (latent_out, clip_loss, grad_mine)


def solution(mesh):
    return jax.shard_map(
        per_device,
        mesh=mesh,
        in_specs=(
            P("dp", None, "seq", None, None),
            P("dp", None),
            P("dp", None),
            P("dp", None),
            P("dp", "seq", None, None),
            P(),
            P(),
            P("dp", "seq", None),
            P("dp", "seq", None),
            P("dp", "seq", None),
            P(),
        ),
        out_specs=(P("dp", None, "seq", None), P("dp", None), P("seq", None)),
        check_vma=False,
    )
```

```python
import jax
import jax.numpy as jnp
from jax import lax
from jax.sharding import PartitionSpec as P

LAT = 64
CLIPS = 4


def with_halo(cells, sides, width):
    for axis, dim in sides:
        count = lax.axis_size(axis)
        ends = count - 1
        head = lax.slice_in_dim(cells, 0, width, axis=dim)
        tail = lax.slice_in_dim(cells, cells.shape[dim] - width, cells.shape[dim], axis=dim)
        cells = jnp.concatenate(
            [
                lax.ppermute(tail, axis, [(i, (i + 1) % count) for i in range(ends)]),
                cells,
                lax.ppermute(head, axis, [((i + 1) % count, i) for i in range(ends)]),
            ],
            axis=dim,
        )
    return cells


def causal_conv(rimmed, conv_weight, keep):
    nframes = rimmed.shape[0]
    chans = rimmed.shape[-1]
    padded = jnp.pad(rimmed, ((0, 0), (0, 0), (1, 1), (0, 0)))
    kernel = jnp.transpose(conv_weight, (1, 2, 3, 0, 4)).reshape(3, 3, chans, 3 * chans)
    each = lax.conv_general_dilated(
        padded,
        kernel,
        (1, 1),
        "VALID",
        dimension_numbers=("NHWC", "HWIO", "NHWC"),
        preferred_element_type=jnp.float32,
    )
    total = each[..., :chans]
    for lag in (1, 2):
        part = each[: nframes - lag, ..., lag * chans : (lag + 1) * chans]
        part = jnp.pad(part, ((lag, 0), (0, 0), (0, 0), (0, 0)))
        total = total + part * keep[lag][:, None, None, None]
    return total


def tree_reduce(grad_t, loss_row, nseq, ndp):
    nbits = nseq.bit_length() - 1
    assert nbits >= 1 and 1 << nbits == nseq and ndp & (ndp - 1) == 0
    groups = [2] + [1] * (nbits - 3) if nbits >= 3 else [1] * (nbits - 1)
    lat = grad_t.shape[0]
    share = grad_t.shape[1] // nseq
    lanes = loss_row.shape[0]
    dense = lat * share // lanes
    me = lax.axis_index("seq")
    halves = grad_t.reshape(lat, nseq // 2, 2, share)
    loss_rows = jnp.broadcast_to(loss_row[None, None, :], (nseq // 2, 1, lanes))

    def half(bit):
        part = lax.dynamic_index_in_dim(halves, bit, 2, keepdims=False)
        part = part.transpose(1, 0, 2).reshape(nseq // 2, dense, lanes)
        return jnp.concatenate([part, loss_rows], axis=1)

    bit = me & 1
    send = half(1 - bit)
    got = lax.ppermute(send, "seq", [(i, i ^ 1) for i in range(nseq)])
    halves, send = lax.optimization_barrier((halves, send))
    x = half(bit) + got
    tail = x.shape[1:]
    low = 1
    for width in groups:
        ways = 1 << width
        x = x.reshape((x.shape[0] // ways, ways) + tail)
        digit = (me >> low) & (ways - 1)
        total = lax.dynamic_index_in_dim(x, digit, 1, keepdims=False)
        for step in range(1, ways):
            send = lax.dynamic_index_in_dim(x, digit ^ step, 1, keepdims=False)
            pairs = [(i, i ^ (step << low)) for i in range(nseq)]
            total = total + lax.ppermute(send, "seq", pairs)
        x = total
        low += width
    x = x.reshape(tail)
    for k in range(ndp.bit_length() - 1):
        x = x + lax.ppermute(x, "dp", [(i, i ^ (1 << k)) for i in range(ndp)])
    return x


def per_device(
    frames,
    frame_counts,
    clip_group,
    timesteps,
    owner_map,
    conv_weight,
    w_latent,
    hidden,
    noise,
    teacher,
    w_out,
):
    nseq = lax.axis_size("seq")
    local = frames[0]
    nframes, nrows, width, chans = local.shape
    tok_rows = nrows // 4
    tok_cols = width // 4
    per_frame = nrows * nseq // 4 * tok_cols
    counts = frame_counts[0]
    ends = jnp.cumsum(counts)
    index = jnp.arange(nframes, dtype=jnp.int32)
    clip_of = jnp.sum((index[:, None] >= ends[None, :]).astype(jnp.int32), axis=1)
    clip_hot = (clip_of[:, None] == jnp.arange(CLIPS, dtype=jnp.int32)[None, :]).astype(jnp.int32)
    starts = jnp.sum(clip_hot * (ends - counts)[None, :], axis=1)
    keep = jnp.stack([(index - lag >= starts).astype(jnp.float32) for lag in range(3)])
    rimmed = with_halo(frames, (("seq", 2),), 1)[0]
    conv = causal_conv(rimmed, conv_weight, keep)
    cells = (local.astype(jnp.float32) + jax.nn.silu(conv)).astype(jnp.bfloat16)
    tokens = lax.conv_general_dilated(
        cells,
        w_latent.reshape(4, 4, chans, LAT),
        (4, 4),
        "VALID",
        dimension_numbers=("NHWC", "HWIO", "NHWC"),
        preferred_element_type=jnp.float32,
    ).astype(jnp.bfloat16)
    latent_out = tokens.reshape(1, nframes, tok_rows, tok_cols * LAT)
    tokens = tokens.reshape(-1, LAT)
    slots = hidden.shape[1]
    capacity = slots // nseq
    assert capacity <= LAT
    owners = owner_map.reshape(-1)
    owner_hot = (owners[:, None] == jnp.arange(nseq, dtype=jnp.int32)[None, :]).astype(jnp.int32)
    ntok = owners.shape[0]
    upto = (jnp.arange(ntok)[:, None] >= jnp.arange(ntok)[None, :]).astype(jnp.bfloat16)
    running = jnp.dot(upto, owner_hot.astype(jnp.bfloat16), preferred_element_type=jnp.float32)
    rank = jnp.sum(running * owner_hot.astype(jnp.float32), axis=1).astype(jnp.int32) - 1
    dest = owners * capacity + rank
    select = (dest[None, :] == jnp.arange(slots, dtype=jnp.int32)[:, None]).astype(jnp.bfloat16)
    tok_clip = jnp.repeat(clip_of, tok_rows * tok_cols).astype(jnp.float32) + 1.0
    outgoing = (
        jnp.dot(select, tokens, preferred_element_type=jnp.float32)
        .astype(jnp.bfloat16)
        .reshape(nseq, capacity, LAT)
    )
    labels = (
        jnp.dot(select, tok_clip.astype(jnp.bfloat16)[:, None], preferred_element_type=jnp.float32)
        .astype(jnp.bfloat16)
        .reshape(nseq, 1, capacity)
    )
    labels = jnp.pad(labels, ((0, 0), (0, 0), (0, LAT - capacity)))
    arrived = lax.all_to_all(
        jnp.concatenate([outgoing, labels], axis=1), "seq", split_axis=0, concat_axis=0, tiled=True
    )
    x0 = arrived[:, :capacity].reshape(slots, LAT).astype(jnp.float32)
    tag = arrived[:, capacity, :capacity].reshape(slots).astype(jnp.float32)
    kind = clip_group[0].astype(jnp.float32)
    coef = (
        (2.0 * kind - 1.0)
        * (0.1 + timesteps[0].astype(jnp.float32) / 1000.0)
        / (counts.astype(jnp.float32) * per_frame)
    )
    slot_hot = (tag[:, None] == (jnp.arange(CLIPS, dtype=jnp.float32) + 1.0)[None, :]).astype(
        jnp.float32
    )
    slot_coef = jnp.sum(slot_hot * coef[None, :], axis=1)
    slot_kind = jnp.sum(slot_hot * kind[None, :], axis=1)
    states = hidden[0].astype(jnp.float32)
    mean = jnp.mean(states, axis=1, keepdims=True)
    centred = states - mean
    var = jnp.mean(centred * centred, axis=1, keepdims=True)
    normed = (centred * lax.rsqrt(var + 1e-06)).astype(jnp.bfloat16)
    pred = jnp.dot(normed, w_out, preferred_element_type=jnp.float32)
    target = slot_kind[:, None] * teacher[0] + (1.0 - slot_kind[:, None]) * (noise[0] - x0)
    diff = pred - target
    err = jnp.sum(diff * diff, axis=1)
    partial_loss = coef * jnp.sum(slot_hot * err[:, None], axis=0)
    dpred = (2.0 * slot_coef[:, None] * diff).astype(jnp.bfloat16)
    states_t = hidden[0].T.astype(jnp.float32)
    normed_t = ((states_t - mean.T) * lax.rsqrt(var.T + 1e-06)).astype(jnp.bfloat16)
    grad_t = lax.dot_general(
        dpred, normed_t, (((0,), (1,)), ((), ())), preferred_element_type=jnp.float32
    )
    ndp = lax.axis_size("dp")
    share = grad_t.shape[1] // nseq
    lanes = 128
    dense = LAT * share // lanes
    assert ndp * CLIPS <= lanes and dense * lanes == LAT * share
    place = lax.axis_index("dp") * CLIPS
    loss_row = lax.dynamic_update_slice(jnp.zeros((lanes,), jnp.float32), partial_loss, (place,))
    summed = tree_reduce(grad_t, loss_row, nseq, ndp)
    grad_mine = summed[:dense].reshape(LAT, share).T
    clip_loss = lax.dynamic_slice_in_dim(summed[dense], place, CLIPS).reshape(1, CLIPS)
    return (latent_out, clip_loss, grad_mine)


def solution(mesh):
    return jax.shard_map(
        per_device,
        mesh=mesh,
        in_specs=(
            P("dp", None, "seq", None, None),
            P("dp", None),
            P("dp", None),
            P("dp", None),
            P("dp", "seq", None, None),
            P(),
            P(),
            P("dp", "seq", None),
            P("dp", "seq", None),
            P("dp", "seq", None),
            P(),
        ),
        out_specs=(P("dp", None, "seq", None), P("dp", None), P("seq", None)),
        check_vma=False,
    )
```

```python
import jax
import jax.numpy as jnp
from jax import lax
from jax.sharding import PartitionSpec as P

LAT = 64
CLIPS = 4


def with_halo(cells, sides, width):
    for axis, dim in sides:
        count = lax.axis_size(axis)
        ends = count - 1
        head = lax.slice_in_dim(cells, 0, width, axis=dim)
        tail = lax.slice_in_dim(cells, cells.shape[dim] - width, cells.shape[dim], axis=dim)
        cells = jnp.concatenate(
            [
                lax.ppermute(tail, axis, [(i, (i + 1) % count) for i in range(ends)]),
                cells,
                lax.ppermute(head, axis, [((i + 1) % count, i) for i in range(ends)]),
            ],
            axis=dim,
        )
    return cells


def causal_conv(rimmed, conv_weight, keep):
    nframes = rimmed.shape[0]
    chans = rimmed.shape[-1]
    padded = jnp.pad(rimmed, ((0, 0), (0, 0), (1, 1), (0, 0)))
    kernel = jnp.transpose(conv_weight, (1, 2, 3, 0, 4)).reshape(3, 3, chans, 3 * chans)
    each = lax.conv_general_dilated(
        padded,
        kernel,
        (1, 1),
        "VALID",
        dimension_numbers=("NHWC", "HWIO", "NHWC"),
        preferred_element_type=jnp.float32,
    )
    total = each[..., :chans]
    for lag in (1, 2):
        part = each[: nframes - lag, ..., lag * chans : (lag + 1) * chans]
        part = jnp.pad(part, ((lag, 0), (0, 0), (0, 0), (0, 0)))
        total = total + part * keep[lag][:, None, None, None]
    return total


def tree_reduce(grad_t, loss_row, nseq, ndp):
    nbits = nseq.bit_length() - 1
    assert nbits >= 1 and 1 << nbits == nseq and ndp & (ndp - 1) == 0
    groups = [2] + [1] * (nbits - 3) if nbits >= 3 else [1] * (nbits - 1)
    lat = grad_t.shape[0]
    share = grad_t.shape[1] // nseq
    lanes = loss_row.shape[0]
    dense = lat * share // lanes
    me = lax.axis_index("seq")
    halves = grad_t.reshape(lat, nseq // 2, 2, share)
    loss_rows = jnp.broadcast_to(loss_row[None, None, :], (nseq // 2, 1, lanes))

    def half(bit):
        part = lax.dynamic_index_in_dim(halves, bit, 2, keepdims=False)
        part = part.transpose(1, 0, 2).reshape(nseq // 2, dense, lanes)
        return jnp.concatenate([part, loss_rows], axis=1)

    bit = me & 1
    send = half(1 - bit)
    got = lax.ppermute(send, "seq", [(i, i ^ 1) for i in range(nseq)])
    halves, send = lax.optimization_barrier((halves, send))
    x = half(bit) + got
    tail = x.shape[1:]
    low = 1
    for width in groups:
        ways = 1 << width
        x = x.reshape((x.shape[0] // ways, ways) + tail)
        digit = (me >> low) & (ways - 1)
        total = lax.dynamic_index_in_dim(x, digit, 1, keepdims=False)
        for step in range(1, ways):
            send = lax.dynamic_index_in_dim(x, digit ^ step, 1, keepdims=False)
            pairs = [(i, i ^ (step << low)) for i in range(nseq)]
            total = total + lax.ppermute(send, "seq", pairs)
        x = total
        low += width
    x = x.reshape(tail)
    group_sum = x
    for k in range(ndp.bit_length() - 1):
        x = x + lax.ppermute(x, "dp", [(i, i ^ (1 << k)) for i in range(ndp)])
    return x, group_sum


def per_device(
    frames,
    frame_counts,
    clip_group,
    timesteps,
    owner_map,
    conv_weight,
    w_latent,
    hidden,
    noise,
    teacher,
    w_out,
):
    nseq = lax.axis_size("seq")
    local = frames[0]
    nframes, nrows, width, chans = local.shape
    tok_rows = nrows // 4
    tok_cols = width // 4
    per_frame = nrows * nseq // 4 * tok_cols
    counts = frame_counts[0]
    ends = jnp.cumsum(counts)
    index = jnp.arange(nframes, dtype=jnp.int32)
    clip_of = jnp.sum((index[:, None] >= ends[None, :]).astype(jnp.int32), axis=1)
    clip_hot = (clip_of[:, None] == jnp.arange(CLIPS, dtype=jnp.int32)[None, :]).astype(jnp.int32)
    starts = jnp.sum(clip_hot * (ends - counts)[None, :], axis=1)
    keep = jnp.stack([(index - lag >= starts).astype(jnp.float32) for lag in range(3)])
    rimmed = with_halo(frames, (("seq", 2),), 1)[0]
    conv = causal_conv(rimmed, conv_weight, keep)
    cells = (local.astype(jnp.float32) + jax.nn.silu(conv)).astype(jnp.bfloat16)
    tokens = lax.conv_general_dilated(
        cells,
        w_latent.reshape(4, 4, chans, LAT),
        (4, 4),
        "VALID",
        dimension_numbers=("NHWC", "HWIO", "NHWC"),
        preferred_element_type=jnp.float32,
    ).astype(jnp.bfloat16)
    latent_out = tokens.reshape(1, nframes, tok_rows, tok_cols * LAT)
    tokens = tokens.reshape(-1, LAT)
    slots = hidden.shape[1]
    capacity = slots // nseq
    assert capacity <= LAT
    owners = owner_map.reshape(-1)
    owner_hot = (owners[:, None] == jnp.arange(nseq, dtype=jnp.int32)[None, :]).astype(jnp.int32)
    ntok = owners.shape[0]
    upto = (jnp.arange(ntok)[:, None] >= jnp.arange(ntok)[None, :]).astype(jnp.bfloat16)
    running = jnp.dot(upto, owner_hot.astype(jnp.bfloat16), preferred_element_type=jnp.float32)
    rank = jnp.sum(running * owner_hot.astype(jnp.float32), axis=1).astype(jnp.int32) - 1
    dest = owners * capacity + rank
    select = (dest[None, :] == jnp.arange(slots, dtype=jnp.int32)[:, None]).astype(jnp.bfloat16)
    tok_clip = jnp.repeat(clip_of, tok_rows * tok_cols).astype(jnp.float32) + 1.0
    outgoing = (
        jnp.dot(select, tokens, preferred_element_type=jnp.float32)
        .astype(jnp.bfloat16)
        .reshape(nseq, capacity, LAT)
    )
    labels = (
        jnp.dot(select, tok_clip.astype(jnp.bfloat16)[:, None], preferred_element_type=jnp.float32)
        .astype(jnp.bfloat16)
        .reshape(nseq, 1, capacity)
    )
    labels = jnp.pad(labels, ((0, 0), (0, 0), (0, LAT - capacity)))
    arrived = lax.all_to_all(
        jnp.concatenate([outgoing, labels], axis=1), "seq", split_axis=0, concat_axis=0, tiled=True
    )
    x0 = arrived[:, :capacity].reshape(slots, LAT).astype(jnp.float32)
    tag = arrived[:, capacity, :capacity].reshape(slots).astype(jnp.float32)
    kind = clip_group[0].astype(jnp.float32)
    coef = (
        (2.0 * kind - 1.0)
        * (0.1 + timesteps[0].astype(jnp.float32) / 1000.0)
        / (counts.astype(jnp.float32) * per_frame)
    )
    slot_hot = (tag[:, None] == (jnp.arange(CLIPS, dtype=jnp.float32) + 1.0)[None, :]).astype(
        jnp.float32
    )
    slot_coef = jnp.sum(slot_hot * coef[None, :], axis=1)
    slot_kind = jnp.sum(slot_hot * kind[None, :], axis=1)
    states = hidden[0].astype(jnp.float32)
    mean = jnp.mean(states, axis=1, keepdims=True)
    centred = states - mean
    var = jnp.mean(centred * centred, axis=1, keepdims=True)
    normed = (centred * lax.rsqrt(var + 1e-06)).astype(jnp.bfloat16)
    pred = jnp.dot(normed, w_out, preferred_element_type=jnp.float32)
    target = slot_kind[:, None] * teacher[0] + (1.0 - slot_kind[:, None]) * (noise[0] - x0)
    diff = pred - target
    err = jnp.sum(diff * diff, axis=1)
    partial_loss = coef * jnp.sum(slot_hot * err[:, None], axis=0)
    dpred = (2.0 * slot_coef[:, None] * diff).astype(jnp.bfloat16)
    states_t = hidden[0].T.astype(jnp.float32)
    normed_t = ((states_t - mean.T) * lax.rsqrt(var.T + 1e-06)).astype(jnp.bfloat16)
    grad_t = lax.dot_general(
        dpred, normed_t, (((0,), (1,)), ((), ())), preferred_element_type=jnp.float32
    )
    ndp = lax.axis_size("dp")
    share = grad_t.shape[1] // nseq
    lanes = 128
    dense = LAT * share // lanes
    assert dense * lanes == LAT * share
    loss_row = jnp.pad(partial_loss, (0, lanes - CLIPS))
    summed, group_sum = tree_reduce(grad_t, loss_row, nseq, ndp)
    grad_mine = summed[:dense].reshape(LAT, share).T
    clip_loss = group_sum[dense, :CLIPS].reshape(1, CLIPS)
    return (latent_out, clip_loss, grad_mine)


def solution(mesh):
    return jax.shard_map(
        per_device,
        mesh=mesh,
        in_specs=(
            P("dp", None, "seq", None, None),
            P("dp", None),
            P("dp", None),
            P("dp", None),
            P("dp", "seq", None, None),
            P(),
            P(),
            P("dp", "seq", None),
            P("dp", "seq", None),
            P("dp", "seq", None),
            P(),
        ),
        out_specs=(P("dp", None, "seq", None), P("dp", None), P("seq", None)),
        check_vma=False,
    )
```

```python
import jax
import jax.numpy as jnp
from jax import lax
from jax.sharding import PartitionSpec as P

LAT = 64
CLIPS = 4


def with_halo(cells, sides, width):
    for axis, dim in sides:
        count = lax.axis_size(axis)
        ends = count - 1
        head = lax.slice_in_dim(cells, 0, width, axis=dim)
        tail = lax.slice_in_dim(cells, cells.shape[dim] - width, cells.shape[dim], axis=dim)
        cells = jnp.concatenate(
            [
                lax.ppermute(tail, axis, [(i, (i + 1) % count) for i in range(ends)]),
                cells,
                lax.ppermute(head, axis, [((i + 1) % count, i) for i in range(ends)]),
            ],
            axis=dim,
        )
    return cells


def causal_conv(rimmed, conv_weight, keep):
    nframes = rimmed.shape[0]
    chans = rimmed.shape[-1]
    padded = jnp.pad(rimmed, ((0, 0), (0, 0), (1, 1), (0, 0)))
    kernel = jnp.transpose(conv_weight, (1, 2, 3, 0, 4)).reshape(3, 3, chans, 3 * chans)
    each = lax.conv_general_dilated(
        padded,
        kernel,
        (1, 1),
        "VALID",
        dimension_numbers=("NHWC", "HWIO", "NHWC"),
        preferred_element_type=jnp.float32,
    )
    total = each[..., :chans]
    for lag in (1, 2):
        part = each[: nframes - lag, ..., lag * chans : (lag + 1) * chans]
        part = jnp.pad(part, ((lag, 0), (0, 0), (0, 0), (0, 0)))
        total = total + part * keep[lag][:, None, None, None]
    return total


def tree_reduce(grad_t, loss_row, nseq, ndp):
    nbits = nseq.bit_length() - 1
    assert nbits >= 1 and 1 << nbits == nseq and ndp & (ndp - 1) == 0
    groups = [2] + [1] * (nbits - 3) if nbits >= 3 else [1] * (nbits - 1)
    lat = grad_t.shape[0]
    share = grad_t.shape[1] // nseq
    lanes = loss_row.shape[0]
    dense = lat * share // lanes
    me = lax.axis_index("seq")
    halves = grad_t.reshape(lat, nseq // 2, 2, share)
    loss_rows = jnp.broadcast_to(loss_row[None, None, :], (nseq // 2, 1, lanes))

    def half(bit):
        part = lax.dynamic_index_in_dim(halves, bit, 2, keepdims=False)
        part = part.transpose(1, 0, 2).reshape(nseq // 2, dense, lanes)
        return jnp.concatenate([part, loss_rows], axis=1)

    bit = me & 1
    send = half(1 - bit)
    got = lax.ppermute(send, "seq", [(i, i ^ 1) for i in range(nseq)])
    halves, send = lax.optimization_barrier((halves, send))
    x = half(bit) + got
    tail = x.shape[1:]
    low = 1
    for width in groups:
        ways = 1 << width
        x = x.reshape((x.shape[0] // ways, ways) + tail)
        digit = (me >> low) & (ways - 1)
        total = lax.dynamic_index_in_dim(x, digit, 1, keepdims=False)
        for step in range(ways - 1, 0, -1):
            send = lax.dynamic_index_in_dim(x, digit ^ step, 1, keepdims=False)
            pairs = [(i, i ^ (step << low)) for i in range(nseq)]
            total = total + lax.ppermute(send, "seq", pairs)
        x = total
        low += width
    x = x.reshape(tail)
    group_sum = x
    for k in range(ndp.bit_length() - 1):
        x = x + lax.ppermute(x, "dp", [(i, i ^ (1 << k)) for i in range(ndp)])
    return x, group_sum


def per_device(
    frames,
    frame_counts,
    clip_group,
    timesteps,
    owner_map,
    conv_weight,
    w_latent,
    hidden,
    noise,
    teacher,
    w_out,
):
    nseq = lax.axis_size("seq")
    local = frames[0]
    nframes, nrows, width, chans = local.shape
    tok_rows = nrows // 4
    tok_cols = width // 4
    per_frame = nrows * nseq // 4 * tok_cols
    counts = frame_counts[0]
    ends = jnp.cumsum(counts)
    index = jnp.arange(nframes, dtype=jnp.int32)
    clip_of = jnp.sum((index[:, None] >= ends[None, :]).astype(jnp.int32), axis=1)
    clip_hot = (clip_of[:, None] == jnp.arange(CLIPS, dtype=jnp.int32)[None, :]).astype(jnp.int32)
    starts = jnp.sum(clip_hot * (ends - counts)[None, :], axis=1)
    keep = jnp.stack([(index - lag >= starts).astype(jnp.float32) for lag in range(3)])
    rimmed = with_halo(frames, (("seq", 2),), 1)[0]
    conv = causal_conv(rimmed, conv_weight, keep)
    cells = (local.astype(jnp.float32) + jax.nn.silu(conv)).astype(jnp.bfloat16)
    tokens = lax.conv_general_dilated(
        cells,
        w_latent.reshape(4, 4, chans, LAT),
        (4, 4),
        "VALID",
        dimension_numbers=("NHWC", "HWIO", "NHWC"),
        preferred_element_type=jnp.float32,
    ).astype(jnp.bfloat16)
    latent_out = tokens.reshape(1, nframes, tok_rows, tok_cols * LAT)
    tokens = tokens.reshape(-1, LAT)
    slots = hidden.shape[1]
    capacity = slots // nseq
    assert capacity <= LAT
    owners = owner_map.reshape(-1)
    owner_hot = (owners[:, None] == jnp.arange(nseq, dtype=jnp.int32)[None, :]).astype(jnp.int32)
    ntok = owners.shape[0]
    upto = (jnp.arange(ntok)[:, None] >= jnp.arange(ntok)[None, :]).astype(jnp.bfloat16)
    running = jnp.dot(upto, owner_hot.astype(jnp.bfloat16), preferred_element_type=jnp.float32)
    rank = jnp.sum(running * owner_hot.astype(jnp.float32), axis=1).astype(jnp.int32) - 1
    dest = owners * capacity + rank
    select = (dest[None, :] == jnp.arange(slots, dtype=jnp.int32)[:, None]).astype(jnp.bfloat16)
    tok_clip = jnp.repeat(clip_of, tok_rows * tok_cols).astype(jnp.float32) + 1.0
    outgoing = (
        jnp.dot(select, tokens, preferred_element_type=jnp.float32)
        .astype(jnp.bfloat16)
        .reshape(nseq, capacity, LAT)
    )
    labels = (
        jnp.dot(select, tok_clip.astype(jnp.bfloat16)[:, None], preferred_element_type=jnp.float32)
        .astype(jnp.bfloat16)
        .reshape(nseq, 1, capacity)
    )
    labels = jnp.pad(labels, ((0, 0), (0, 0), (0, LAT - capacity)))
    arrived = lax.all_to_all(
        jnp.concatenate([outgoing, labels], axis=1), "seq", split_axis=0, concat_axis=0, tiled=True
    )
    x0 = arrived[:, :capacity].reshape(slots, LAT).astype(jnp.float32)
    tag = arrived[:, capacity, :capacity].reshape(slots).astype(jnp.float32)
    kind = clip_group[0].astype(jnp.float32)
    coef = (
        (2.0 * kind - 1.0)
        * (0.1 + timesteps[0].astype(jnp.float32) / 1000.0)
        / (counts.astype(jnp.float32) * per_frame)
    )
    slot_hot = (tag[:, None] == (jnp.arange(CLIPS, dtype=jnp.float32) + 1.0)[None, :]).astype(
        jnp.float32
    )
    slot_coef = jnp.sum(slot_hot * coef[None, :], axis=1)
    slot_kind = jnp.sum(slot_hot * kind[None, :], axis=1)
    states = hidden[0].astype(jnp.float32)
    mean = jnp.mean(states, axis=1, keepdims=True)
    centred = states - mean
    var = jnp.mean(centred * centred, axis=1, keepdims=True)
    normed = (centred * lax.rsqrt(var + 1e-06)).astype(jnp.bfloat16)
    pred = jnp.dot(normed, w_out, preferred_element_type=jnp.float32)
    target = slot_kind[:, None] * teacher[0] + (1.0 - slot_kind[:, None]) * (noise[0] - x0)
    diff = pred - target
    err = jnp.sum(diff * diff, axis=1)
    partial_loss = coef * jnp.sum(slot_hot * err[:, None], axis=0)
    dpred = (2.0 * slot_coef[:, None] * diff).astype(jnp.bfloat16)
    states_t = hidden[0].T.astype(jnp.float32)
    normed_t = ((states_t - mean.T) * lax.rsqrt(var.T + 1e-06)).astype(jnp.bfloat16)
    grad_t = lax.dot_general(
        dpred, normed_t, (((0,), (1,)), ((), ())), preferred_element_type=jnp.float32
    )
    ndp = lax.axis_size("dp")
    share = grad_t.shape[1] // nseq
    lanes = 128
    dense = LAT * share // lanes
    assert dense * lanes == LAT * share
    loss_row = jnp.pad(partial_loss, (0, lanes - CLIPS))
    summed, group_sum = tree_reduce(grad_t, loss_row, nseq, ndp)
    grad_mine = summed[:dense].reshape(LAT, share).T
    clip_loss = group_sum[dense, :CLIPS].reshape(1, CLIPS)
    return (latent_out, clip_loss, grad_mine)


def solution(mesh):
    return jax.shard_map(
        per_device,
        mesh=mesh,
        in_specs=(
            P("dp", None, "seq", None, None),
            P("dp", None),
            P("dp", None),
            P("dp", None),
            P("dp", "seq", None, None),
            P(),
            P(),
            P("dp", "seq", None),
            P("dp", "seq", None),
            P("dp", "seq", None),
            P(),
        ),
        out_specs=(P("dp", None, "seq", None), P("dp", None), P("seq", None)),
        check_vma=False,
    )
```

```python
import jax
import jax.numpy as jnp
from jax import lax
from jax.sharding import PartitionSpec as P

LAT = 64
CLIPS = 4


def with_halo(cells, sides, width):
    for axis, dim in sides:
        count = lax.axis_size(axis)
        ends = count - 1
        head = lax.slice_in_dim(cells, 0, width, axis=dim)
        tail = lax.slice_in_dim(cells, cells.shape[dim] - width, cells.shape[dim], axis=dim)
        cells = jnp.concatenate(
            [
                lax.ppermute(tail, axis, [(i, (i + 1) % count) for i in range(ends)]),
                cells,
                lax.ppermute(head, axis, [((i + 1) % count, i) for i in range(ends)]),
            ],
            axis=dim,
        )
    return cells


def causal_conv(rimmed, conv_weight, keep):
    nframes = rimmed.shape[0]
    chans = rimmed.shape[-1]
    padded = jnp.pad(rimmed, ((0, 0), (0, 0), (1, 1), (0, 0)))
    kernel = jnp.transpose(conv_weight, (1, 2, 3, 0, 4)).reshape(3, 3, chans, 3 * chans)
    each = lax.conv_general_dilated(
        padded,
        kernel,
        (1, 1),
        "VALID",
        dimension_numbers=("NHWC", "HWIO", "NHWC"),
        preferred_element_type=jnp.float32,
    )
    total = each[..., :chans]
    for lag in (1, 2):
        part = each[: nframes - lag, ..., lag * chans : (lag + 1) * chans]
        part = jnp.pad(part, ((lag, 0), (0, 0), (0, 0), (0, 0)))
        total = total + part * keep[lag][:, None, None, None]
    return total


def tree_reduce(grad_t, loss_row, nseq, ndp):
    nbits = nseq.bit_length() - 1
    assert nbits >= 1 and 1 << nbits == nseq and ndp & (ndp - 1) == 0
    groups = [2] + [1] * (nbits - 3) if nbits >= 3 else [1] * (nbits - 1)
    lat = grad_t.shape[0]
    share = grad_t.shape[1] // nseq
    lanes = loss_row.shape[0]
    dense = lat * share // lanes
    me = lax.axis_index("seq")
    halves = grad_t.reshape(lat, nseq // 2, 2, share)
    loss_rows = jnp.broadcast_to(loss_row[None, None, :], (nseq // 2, 1, lanes))

    def half(bit):
        part = lax.dynamic_index_in_dim(halves, bit, 2, keepdims=False)
        part = part.transpose(1, 0, 2).reshape(nseq // 2, dense, lanes)
        return jnp.concatenate([part, loss_rows], axis=1)

    bit = me & 1
    send = half(1 - bit)
    got = lax.ppermute(send, "seq", [(i, i ^ 1) for i in range(nseq)])
    halves, send = lax.optimization_barrier((halves, send))
    x = half(bit) + got
    tail = x.shape[1:]
    low = 1
    for width in groups:
        ways = 1 << width
        x = x.reshape((x.shape[0] // ways, ways) + tail)
        digit = (me >> low) & (ways - 1)
        total = lax.dynamic_index_in_dim(x, digit, 1, keepdims=False)
        for step in range(ways - 1, 0, -1):
            send = lax.dynamic_index_in_dim(x, digit ^ step, 1, keepdims=False)
            pairs = [(i, i ^ (step << low)) for i in range(nseq)]
            total = total + lax.ppermute(send, "seq", pairs)
        x = total
        low += width
    x = x.reshape(tail)
    group_sum = x
    for k in range(ndp.bit_length() - 1):
        x = x + lax.ppermute(x, "dp", [(i, i ^ (1 << k)) for i in range(ndp)])
    return x, group_sum


def per_device(
    frames,
    frame_counts,
    clip_group,
    timesteps,
    owner_map,
    conv_weight,
    w_latent,
    hidden,
    noise,
    teacher,
    w_out,
):
    nseq = lax.axis_size("seq")
    local = frames[0]
    nframes, nrows, width, chans = local.shape
    tok_rows = nrows // 4
    tok_cols = width // 4
    per_frame = nrows * nseq // 4 * tok_cols
    counts = frame_counts[0]
    ends = jnp.cumsum(counts)
    index = jnp.arange(nframes, dtype=jnp.int32)
    clip_of = jnp.sum((index[:, None] >= ends[None, :]).astype(jnp.int32), axis=1)
    clip_hot = (clip_of[:, None] == jnp.arange(CLIPS, dtype=jnp.int32)[None, :]).astype(jnp.int32)
    starts = jnp.sum(clip_hot * (ends - counts)[None, :], axis=1)
    keep = jnp.stack([(index - lag >= starts).astype(jnp.float32) for lag in range(3)])
    rimmed = with_halo(frames, (("seq", 2),), 1)[0]
    conv = causal_conv(rimmed, conv_weight, keep)
    cells = (local.astype(jnp.float32) + jax.nn.silu(conv)).astype(jnp.bfloat16)
    tokens = lax.conv_general_dilated(
        cells,
        w_latent.reshape(4, 4, chans, LAT),
        (4, 4),
        "VALID",
        dimension_numbers=("NHWC", "HWIO", "NHWC"),
        preferred_element_type=jnp.float32,
    ).astype(jnp.bfloat16)
    latent_out = tokens.reshape(1, nframes, tok_rows, tok_cols * LAT)
    tokens = tokens.reshape(-1, LAT)
    slots = hidden.shape[1]
    capacity = slots // nseq
    assert capacity <= LAT
    owners = owner_map.reshape(-1)
    owner_hot = (owners[:, None] == jnp.arange(nseq, dtype=jnp.int32)[None, :]).astype(jnp.int32)
    ntok = owners.shape[0]
    upto = (jnp.arange(ntok)[:, None] >= jnp.arange(ntok)[None, :]).astype(jnp.bfloat16)
    running = jnp.dot(upto, owner_hot.astype(jnp.bfloat16), preferred_element_type=jnp.float32)
    rank = jnp.sum(running * owner_hot.astype(jnp.float32), axis=1).astype(jnp.int32) - 1
    dest = owners * capacity + rank
    select = (dest[None, :] == jnp.arange(slots, dtype=jnp.int32)[:, None]).astype(jnp.bfloat16)
    tok_clip = jnp.repeat(clip_of, tok_rows * tok_cols).astype(jnp.float32) + 1.0
    outgoing = jnp.dot(select, tokens, preferred_element_type=jnp.float32).reshape(
        nseq, capacity, LAT
    )
    labels = jnp.dot(
        select, tok_clip.astype(jnp.bfloat16)[:, None], preferred_element_type=jnp.float32
    ).reshape(nseq, 1, capacity)
    labels = jnp.pad(labels, ((0, 0), (0, 0), (0, LAT - capacity)))
    arrived = lax.all_to_all(
        jnp.concatenate([outgoing, labels], axis=1), "seq", split_axis=0, concat_axis=0, tiled=True
    )
    x0 = arrived[:, :capacity].reshape(slots, LAT).astype(jnp.float32)
    tag = arrived[:, capacity, :capacity].reshape(slots).astype(jnp.float32)
    kind = clip_group[0].astype(jnp.float32)
    coef = (
        (2.0 * kind - 1.0)
        * (0.1 + timesteps[0].astype(jnp.float32) / 1000.0)
        / (counts.astype(jnp.float32) * per_frame)
    )
    slot_hot = (tag[:, None] == (jnp.arange(CLIPS, dtype=jnp.float32) + 1.0)[None, :]).astype(
        jnp.float32
    )
    slot_coef = jnp.sum(slot_hot * coef[None, :], axis=1)
    slot_kind = jnp.sum(slot_hot * kind[None, :], axis=1)
    states = hidden[0].astype(jnp.float32)
    mean = jnp.mean(states, axis=1, keepdims=True)
    centred = states - mean
    var = jnp.mean(centred * centred, axis=1, keepdims=True)
    normed = (centred * lax.rsqrt(var + 1e-06)).astype(jnp.bfloat16)
    pred = jnp.dot(normed, w_out, preferred_element_type=jnp.float32)
    target = slot_kind[:, None] * teacher[0] + (1.0 - slot_kind[:, None]) * (noise[0] - x0)
    diff = pred - target
    err = jnp.sum(diff * diff, axis=1)
    partial_loss = coef * jnp.sum(slot_hot * err[:, None], axis=0)
    dpred = (2.0 * slot_coef[:, None] * diff).astype(jnp.bfloat16)
    states_t = hidden[0].T.astype(jnp.float32)
    normed_t = ((states_t - mean.T) * lax.rsqrt(var.T + 1e-06)).astype(jnp.bfloat16)
    grad_t = lax.dot_general(
        dpred, normed_t, (((0,), (1,)), ((), ())), preferred_element_type=jnp.float32
    )
    ndp = lax.axis_size("dp")
    share = grad_t.shape[1] // nseq
    lanes = 128
    dense = LAT * share // lanes
    assert dense * lanes == LAT * share
    loss_row = jnp.pad(partial_loss, (0, lanes - CLIPS))
    summed, group_sum = tree_reduce(grad_t, loss_row, nseq, ndp)
    grad_mine = summed[:dense].reshape(LAT, share).T
    clip_loss = group_sum[dense, :CLIPS].reshape(1, CLIPS)
    return (latent_out, clip_loss, grad_mine)


def solution(mesh):
    return jax.shard_map(
        per_device,
        mesh=mesh,
        in_specs=(
            P("dp", None, "seq", None, None),
            P("dp", None),
            P("dp", None),
            P("dp", None),
            P("dp", "seq", None, None),
            P(),
            P(),
            P("dp", "seq", None),
            P("dp", "seq", None),
            P("dp", "seq", None),
            P(),
        ),
        out_specs=(P("dp", None, "seq", None), P("dp", None), P("seq", None)),
        check_vma=False,
    )
```
